512 devices in a mesh: dp: 8 (over x, core), expert: 64 (over z, y).
Axes of the slice: x: 4, y: 8, z: 8, core: 2. Of those that a mesh axis runs over, the one named last changes fastest.
Arguments:
- tokens: bfloat16 [65536, 512], P(('dp', 'expert')), may hold values from -6 to 6
- modality: int32 [65536], P(('dp', 'expert')), may hold values 0 or 1
- modal_gains: float32 [2, 512], replicated, may hold values from 0.5 to 2
- routes: int32 [65536, 2], P(('dp', 'expert')), may hold values from 0 to 63, all different within a row; in each aligned block of 128 rows (0 to 127, 128 to 255, ...) at most 8 rows name the same one
- gate_share: int32 [65536], P(('dp', 'expert')), may hold values from 1 to 15
- up_weight: bfloat16 [64, 2048, 512], P('expert', 'dp'), may hold values from -0.25 to 0.25
- down_weight: bfloat16 [64, 2048, 512], P('expert', 'dp'), may hold values from -0.125 to 0.125
- cotangent: bfloat16 [65536, 512], P(('dp', 'expert')), may hold values from -6 to 6
Outputs:
- moe_output: bfloat16 [65536, 512], P(('dp', 'expert'))
- token_grad: bfloat16 [65536, 512], P(('dp', 'expert'))
- up_grad: bfloat16 [64, 2048, 512], P('expert', 'dp')
- down_grad: bfloat16 [64, 2048, 512], P('expert', 'dp')
The draws below stay inside these ranges and needn't reach their ends.
Inputs may be any that keep to these rules, and one draw needn't show every extreme that they name: `routes`: each row names two different experts; among the 128 rows of one device no expert is named more than 8 times, and in every draw some device names some expert exactly 8 times.
All inputs are finite; a program needn't handle non-finite values. No bound on the sum of `modality` on one device may be relied on, other than what follows from the above.
Results may differ from the reference program's by a relative error of at most 0.014.
Values may be sent and summed in bfloat16 or wider, within the bound.
No kernel may reach another device: no remote copies, remote signals or barrier semaphores. Data moves between devices by JAX's collectives and lax.ppermute only.
A program may use at most 64 MiB of HBM per device.

```python
import math
import jax
import jax.numpy as jnp
import numpy as np
from jax import lax

D = 512
FF = 2048
TOK_DEV = 128
EXPERTS = 64
CAP = 8
SLOTS = 512
GROUP_TOKENS = 8192
TOKENS = 65536
ROUTES_EXPERT = 2048
N_DP = 8


def with_ends(result, rng, least, top_value):
    shape = result.shape
    place = [jax.random.randint(jax.random.fold_in(rng, axis), (), 0, shape[axis]) for axis in range(len(shape))]
    result = result.at[tuple(place)].set(least)
    longest = shape.index(max(shape))
    place[longest] = (place[longest] + 1) % shape[longest]
    return result.at[tuple(place)].set(top_value)


def steps_of(own_key, shape, pieces, least, high):
    factor_of, own = 1.0, jax.random.fold_in(own_key, 6)
    for dim, parts in pieces:
        steps = jnp.exp(jax.random.uniform(jax.random.fold_in(own, dim), (parts,), jnp.float32, least / len(pieces), high / len(pieces)))
        factor_of = factor_of * jnp.repeat(steps, shape[dim] // parts).reshape([-1 if axis == dim else 1 for axis in range(len(shape))])
    return factor_of


def routed_block(own_key, own, number, rows, number_of, top, most, lean):
    order = jax.random.permutation(own_key, number_of)
    heavy_load, common = shares(number_of, rows * top, most, lean, True), shares(number_of, rows * top, most, lean, False)
    places = jnp.arange(number_of)

    def named(sizes, offset_by):
        used = int((sizes > 0).sum())
        fixed = max(1, used // 4)
        shifted = fixed + (places - fixed + offset_by * (used - fixed)) % max(1, number_of - fixed)
        return jnp.zeros((number_of,), jnp.int32).at[order[jnp.where(places < fixed, places, shifted)]].set(jnp.asarray(sizes, jnp.int32))

    sizes = jnp.where(number % 4 == 0, named(heavy_load, number // 4), named(common, number - number // 4 - 1))
    mixed = jax.random.permutation(jax.random.fold_in(own, 3), number_of)
    donor, receiver = mixed[0:number_of // 2 * 2:2], mixed[1:number_of // 2 * 2:2]
    margin = jnp.minimum(sizes[donor] - 1, most - sizes[receiver]) // 2
    margin = jnp.where((donor == order[0]) | (receiver == order[0]) | (sizes[receiver] == 0), 0, jnp.maximum(margin, 0))
    shifted = jax.random.randint(jax.random.fold_in(own, 4), (number_of // 2,), 0, 1 << 20) % (margin + 1)
    sizes = sizes.at[donor].add(-shifted).at[receiver].add(shifted)
    items = jnp.searchsorted(jnp.cumsum(sizes), jnp.arange(rows * top), side="right").astype(jnp.int32)
    listing = items.reshape(top, rows).T
    listing = listing[jax.random.permutation(jax.random.fold_in(own, 1), rows)]
    offset_by = jax.random.randint(jax.random.fold_in(own, 2), (rows, 1), 0, top)
    return jnp.take_along_axis(listing, (jnp.arange(top)[None, :] + offset_by) % top, axis=1)


def shares(amount, total, limit, slope, full):
    weights = [(1 << 20) // math.isqrt(standing ** slope) + 1 for standing in range(1, amount + 1)]
    largest = limit if full else min(limit, max(-(-total // amount), total * weights[0] // sum(weights)))
    least = 1 if total - largest >= amount - 1 else 0
    counts, spare = [largest] + [least] * (amount - 1), total - largest - least * (amount - 1)
    while spare > 0:
        candidates = [i for i in range(1, amount) if counts[i] < largest] or [i for i in range(1, amount) if counts[i] < limit]
        mass, left = sum([weights[i] for i in candidates]), spare
        for i in candidates:
            more = min(limit - counts[i], max(1, left * weights[i] // mass), spare)
            counts[i] = counts[i] + more
            spare = spare - more
    return np.array(counts)


def centred(rng, dims, spread, limit, pieces=(), held_as=jnp.bfloat16):
    entries = spread * jax.random.normal(rng, dims, jnp.float32)
    if pieces:
        entries = entries * steps_of(rng, dims, pieces, -0.22, 0.18)
    return jnp.clip(entries, -limit, limit).astype(held_as)


def setup_inputs(seed: int = 0) -> dict:
    arg_keys = jax.random.split(jax.random.key(seed), 9)
    tokens = centred(arg_keys[0], (TOKENS, D), 1.0, 6.0, ((0, 512),))
    modality = with_ends((jax.random.randint(arg_keys[1], (TOKENS,), 0, 2) < 1).astype(jnp.int32), jax.random.fold_in(arg_keys[1], 1), 0, 1)
    modal_gains = jnp.clip(jnp.exp(jax.random.uniform(arg_keys[2], (2, D), jnp.float32, math.log(0.5), math.log(2.0))), 0.5, 2.0)
    routes_keys = jax.random.split(jax.random.fold_in(arg_keys[3], 1), TOKENS // TOK_DEV)
    routes_turns = jax.random.permutation(jax.random.fold_in(arg_keys[3], 3), TOKENS // TOK_DEV)
    routes = jax.vmap(lambda own, number: routed_block(jax.random.fold_in(arg_keys[3], 2), own, number, TOK_DEV, EXPERTS, 2, CAP, 2))(routes_keys, routes_turns).reshape((TOKENS, 2))
    gate_share = with_ends(jax.random.randint(arg_keys[4], (TOKENS,), 1, 16), jax.random.fold_in(arg_keys[4], 1), 1, 15).astype(jnp.int32)
    up_weight = centred(arg_keys[5], (EXPERTS, FF, D), D ** -0.5, 0.25, ((0, 64), (1, 8)))
    down_weight = centred(arg_keys[6], (EXPERTS, FF, D), FF ** -0.5, 0.125, ((0, 64), (1, 8)))
    cotangent = centred(arg_keys[7], (TOKENS, D), 1.0, 6.0, ((0, 512),))
    return {"tokens": tokens, "modality": modality, "modal_gains": modal_gains, "routes": routes, "gate_share": gate_share, "up_weight": up_weight, "down_weight": down_weight, "cotangent": cotangent}


root_half = 0.7071067811865476
density = 0.3989422804014327

def gelu_value(values):
    return values * 0.5 * (1.0 + lax.erf(values * root_half))

def gelu_slope(values):
    return 0.5 * (1.0 + lax.erf(values * root_half)) + values * jnp.exp(-0.5 * values * values) * density

def reference(tokens, modality, modal_gains, routes, gate_share, up_weight, down_weight, cotangent):
    x_float = tokens.astype(jnp.float32)
    inv_rms = lax.rsqrt(lax.optimization_barrier(jnp.mean(x_float * x_float, axis=-1, keepdims=True)) + 1e-06)
    gain_rows = jnp.where(modality[:, None] == 1, modal_gains[1][None, :], modal_gains[0][None, :])
    normed = (x_float * inv_rms * gain_rows).astype(jnp.bfloat16)
    gate_first = gate_share.astype(jnp.float32) / 16.0
    gate_pair = jnp.stack([gate_first, 1.0 - gate_first], axis=1)
    route_grad = (gate_pair[:, :, None] * cotangent.astype(jnp.float32)[:, None, :]).astype(jnp.bfloat16).reshape(-1, D)
    normed_routes = jnp.repeat(normed, 2, axis=0)
    flat_routes = routes.reshape(-1).astype(jnp.int32)
    route_total = flat_routes.shape[0]
    route_ids = jnp.arange(route_total, dtype=jnp.int32)
    group_of = (route_ids // 2 // GROUP_TOKENS).astype(jnp.int32)
    group_key = (group_of * EXPERTS + flat_routes).astype(jnp.int32)
    ordering = jnp.argsort(group_key, stable=True).astype(jnp.int32)
    group_sizes = jax.ops.segment_sum(jnp.ones((route_total,), jnp.int32), group_key, num_segments=N_DP * EXPERTS).astype(jnp.int32)
    group_start = (jnp.cumsum(group_sizes) - group_sizes).astype(jnp.int32)
    rank_sorted = (route_ids - group_start[group_key[ordering]]).astype(jnp.int32)
    route_rank = jnp.zeros((route_total,), jnp.int32).at[ordering].set(rank_sorted)
    slot_ids = jnp.arange(SLOTS, dtype=jnp.int32)
    grad_scale = 1.0 / math.sqrt(ROUTES_EXPERT)

    def per_expert(expert):
        weight_first = up_weight[expert]
        weight_second = down_weight[expert]

        def per_group(totals, group_index):
            group_now = group_index * EXPERTS + expert
            is_valid = slot_ids < group_sizes[group_now]
            picked = ordering[jnp.minimum(group_start[group_now] + slot_ids, route_total - 1)]
            input_rows = jnp.where(is_valid[:, None], normed_routes[picked], jnp.zeros((), jnp.bfloat16))
            grad_rows = jnp.where(is_valid[:, None], route_grad[picked], jnp.zeros((), jnp.bfloat16))
            pre_act = jnp.dot(input_rows, weight_first.T, preferred_element_type=jnp.float32)
            activated = gelu_value(pre_act).astype(jnp.bfloat16)
            expert_rows = jnp.dot(activated, weight_second, preferred_element_type=jnp.float32).astype(jnp.bfloat16)
            hidden_grad = jnp.dot(grad_rows, weight_second.T, preferred_element_type=jnp.float32)
            pre_grad = (hidden_grad * gelu_slope(pre_act)).astype(jnp.bfloat16)
            back_rows = jnp.dot(pre_grad, weight_first, preferred_element_type=jnp.float32).astype(jnp.bfloat16)
            partial_first = (jnp.dot(pre_grad.T, input_rows, preferred_element_type=jnp.float32) * grad_scale).astype(jnp.bfloat16)
            partial_second = (jnp.dot(activated.T, grad_rows, preferred_element_type=jnp.float32) * grad_scale).astype(jnp.bfloat16)
            partial_first, partial_second = lax.optimization_barrier((partial_first, partial_second))
            totals = (totals[0] + partial_first.astype(jnp.float32), totals[1] + partial_second.astype(jnp.float32))
            return (totals, (expert_rows, back_rows))
        zero_grad = jnp.zeros((FF, D), jnp.float32)
        totals, stacked = lax.scan(per_group, (zero_grad, zero_grad), jnp.arange(N_DP, dtype=jnp.int32))
        return (totals[0].astype(jnp.bfloat16), totals[1].astype(jnp.bfloat16), stacked[0], stacked[1])
    up_grad, down_grad, expert_all, back_all = lax.map(per_expert, jnp.arange(EXPERTS, dtype=jnp.int32))
    route_out = expert_all[flat_routes, group_of, route_rank].astype(jnp.float32).reshape(-1, 2, D)
    moe_output = lax.optimization_barrier(jnp.sum(gate_pair[:, :, None] * route_out, axis=1)).astype(jnp.bfloat16)
    normed_grad = lax.optimization_barrier(jnp.sum(back_all[flat_routes, group_of, route_rank].astype(jnp.float32).reshape(-1, 2, D), axis=1))
    scaled = gain_rows * normed_grad
    token_grad = (inv_rms * scaled - x_float * inv_rms ** 3 * lax.optimization_barrier(jnp.mean(x_float * scaled, axis=-1, keepdims=True))).astype(jnp.bfloat16)
    return (moe_output, token_grad, up_grad, down_grad)
```

```python
import math

import jax
import jax.numpy as jnp
from jax import lax
from jax.sharding import PartitionSpec as P

root_half = 0.7071067811865476
density = 0.3989422804014327


def gelu_value(values):
    return values * 0.5 * (1.0 + lax.erf(values * root_half))


def gelu_slope(values):
    return (
        0.5 * (1.0 + lax.erf(values * root_half))
        + values * jnp.exp(-0.5 * values * values) * density
    )


def row_product(left_side, right_side, right_axis):
    numbers = (((1,), (right_axis,)), ((), ()))
    return lax.dot_general(left_side, right_side, numbers, preferred_element_type=jnp.float32)


def row_contract(left_side, right_side):
    numbers = (((0,), (0,)), ((), ()))
    return lax.dot_general(left_side, right_side, numbers, preferred_element_type=jnp.float32)


def exchange(rows, expert_count, capacity):
    model_width = rows.shape[-1]
    moved = lax.all_to_all(
        rows.reshape(expert_count, capacity, model_width), "expert", split_axis=0, concat_axis=0, tiled=True
    )
    return moved.reshape(expert_count * capacity, model_width)


def on_device(tokens, modality, modal_gains, routes, gate_share, up_weight, down_weight, cotangent):
    tok_count = tokens.shape[0]
    model_width = tokens.shape[1]
    expert_count = lax.axis_size("expert")
    replica_count = lax.axis_size("dp")
    capacity = 4 * tok_count // expert_count
    slot_count = expert_count * capacity
    route_count = 2 * tok_count
    grad_scale = 1.0 / math.sqrt(2 * tok_count * replica_count)
    whole = lax.all_gather(jnp.concatenate([up_weight, down_weight], axis=0), "dp", axis=1, tiled=True)
    whole_up, whole_down = whole[0], whole[1]
    x_float = tokens.astype(jnp.float32)
    inv_rms = lax.rsqrt(jnp.mean(x_float * x_float, axis=-1, keepdims=True) + 1e-06)
    gain_rows = jnp.where(modality[:, None] == 1, modal_gains[1][None, :], modal_gains[0][None, :])
    normed = (x_float * inv_rms * gain_rows).astype(jnp.bfloat16)
    gate_first = gate_share.astype(jnp.float32) / 16.0
    flat_routes = routes.reshape(-1)
    one_hot = flat_routes[:, None] == jnp.arange(expert_count, dtype=jnp.int32)[None, :]
    route_ids = jnp.arange(route_count, dtype=jnp.int32)
    before = (route_ids[None, :] < route_ids[:, None]).astype(jnp.bfloat16)
    earlier = jnp.dot(before, one_hot.astype(jnp.bfloat16), preferred_element_type=jnp.float32)
    position = jnp.sum(jnp.where(one_hot, earlier, 0.0), axis=1).astype(jnp.int32)
    slot_index = (flat_routes * capacity + position).reshape(tok_count, 2)
    slot_ids = jnp.arange(slot_count, dtype=jnp.int32)[:, None]
    first_hit = slot_ids == slot_index[:, 0][None, :]
    second_hit = slot_ids == slot_index[:, 1][None, :]
    pick = (first_hit | second_hit).astype(jnp.bfloat16)
    weigh = jnp.where(first_hit, gate_first[None, :], jnp.where(second_hit, 1.0 - gate_first[None, :], 0.0)).astype(
        jnp.bfloat16
    )
    send_rows = jnp.dot(pick, normed, preferred_element_type=jnp.float32).astype(jnp.bfloat16)
    send_grad = jnp.dot(weigh, cotangent, preferred_element_type=jnp.float32).astype(jnp.bfloat16)
    expert_rows = exchange(send_rows, expert_count, capacity)
    grad_rows = exchange(send_grad, expert_count, capacity)
    pre_act = row_product(expert_rows, whole_up, 1)
    activated = gelu_value(pre_act).astype(jnp.bfloat16)
    expert_out = row_product(activated, whole_down, 0).astype(jnp.bfloat16)
    back_rows = exchange(expert_out, expert_count, capacity)
    hidden_grad = row_product(grad_rows, whole_down, 1)
    pre_grad = (hidden_grad * gelu_slope(pre_act)).astype(jnp.bfloat16)
    normed_part = row_product(pre_grad, whole_up, 0).astype(jnp.bfloat16)
    back_grad = exchange(normed_part, expert_count, capacity)
    up_term = row_contract(pre_grad, expert_rows)
    down_term = row_contract(activated, grad_rows)
    grad_pair = lax.psum_scatter(
        (jnp.stack([up_term, down_term], axis=1) * grad_scale).astype(jnp.bfloat16),
        "dp",
        scatter_dimension=0,
        tiled=True,
    ).astype(jnp.float32)
    up_grad = grad_pair[:, 0][None].astype(jnp.bfloat16)
    down_grad = grad_pair[:, 1][None].astype(jnp.bfloat16)
    moe_output = row_contract(weigh, back_rows).astype(jnp.bfloat16)
    normed_grad = row_contract(pick, back_grad)
    scaled = gain_rows * normed_grad
    token_grad = (
        inv_rms * scaled - x_float * inv_rms**3 * jnp.mean(x_float * scaled, axis=-1, keepdims=True)
    ).astype(jnp.bfloat16)
    return (moe_output, token_grad, up_grad, down_grad)


def solution(mesh):
    placed = (
        P(("dp", "expert"), None),
        P(("dp", "expert")),
        P(),
        P(("dp", "expert"), None),
        P(("dp", "expert")),
        P("expert", "dp", None),
        P("expert", "dp", None),
        P(("dp", "expert"), None),
    )
    return jax.shard_map(
        on_device,
        mesh=mesh,
        in_specs=placed,
        out_specs=(
            P(("dp", "expert"), None),
            P(("dp", "expert"), None),
            P("expert", "dp", None),
            P("expert", "dp", None),
        ),
        check_vma=False,
    )
```

```python
import math

import jax
import jax.numpy as jnp
from jax import lax
from jax.sharding import PartitionSpec as P

root_half = 0.7071067811865476
density = 0.3989422804014327


def gelu_value(values):
    return values * 0.5 * (1.0 + lax.erf(values * root_half))


def gelu_slope(values):
    return (
        0.5 * (1.0 + lax.erf(values * root_half))
        + values * jnp.exp(-0.5 * values * values) * density
    )


def row_product(left_side, right_side, right_axis):
    numbers = (((1,), (right_axis,)), ((), ()))
    return lax.dot_general(left_side, right_side, numbers, preferred_element_type=jnp.float32)


def row_contract(left_side, right_side):
    numbers = (((0,), (0,)), ((), ()))
    return lax.dot_general(left_side, right_side, numbers, preferred_element_type=jnp.float32)


def ring_shift(value, chips, cores, shift):
    pairs = [(c * cores + k, ((c + shift) % chips) * cores + k) for c in range(chips) for k in range(cores)]
    return lax.ppermute(value, "dp", pairs)


def core_swap(value, chips, cores):
    pairs = [(c * cores + k, c * cores + (k + 1) % cores) for c in range(chips) for k in range(cores)]
    return lax.ppermute(value, "dp", pairs)


def gather_weights(shard, chips, cores):
    mine = jnp.stack([shard] + [ring_shift(shard, chips, cores, k) for k in range(1, chips)])
    other = core_swap(mine, chips, cores)
    both = jnp.stack([mine, other])
    width = shard.shape[-1]
    up = both[:, :, 0].reshape(-1, width)
    down = both[:, :, 1].reshape(-1, width)
    return up, down


def scatter_grads(parts, chips, cores):
    from_other = core_swap(parts[1], chips, cores)
    summed = parts[0].astype(jnp.float32) + from_other.astype(jnp.float32)
    sent = summed.astype(jnp.bfloat16)
    total = summed[0]
    for k in range(1, chips):
        total = total + ring_shift(sent[k], chips, cores, -k).astype(jnp.float32)
    return total.astype(jnp.bfloat16)


def on_device(tokens, modality, modal_gains, routes, gate_share, up_weight, down_weight, cotangent):
    tok_count = tokens.shape[0]
    model_width = tokens.shape[1]
    expert_count = lax.axis_size("expert")
    replica_count = lax.axis_size("dp")
    cores = 2
    chips = replica_count // cores
    capacity = 4 * tok_count // expert_count
    slot_count = expert_count * capacity
    route_count = 2 * tok_count
    grad_scale = 1.0 / math.sqrt(2 * tok_count * replica_count)
    shard = jnp.concatenate([up_weight, down_weight], axis=0)
    whole_up, whole_down = gather_weights(shard, chips, cores)
    x_float = tokens.astype(jnp.float32)
    inv_rms = lax.rsqrt(jnp.mean(x_float * x_float, axis=-1, keepdims=True) + 1e-06)
    gain_rows = jnp.where(modality[:, None] == 1, modal_gains[1][None, :], modal_gains[0][None, :])
    normed = (x_float * inv_rms * gain_rows).astype(jnp.bfloat16)
    gate_first = gate_share.astype(jnp.float32) / 16.0
    flat_routes = routes.reshape(-1)
    one_hot = flat_routes[:, None] == jnp.arange(expert_count, dtype=jnp.int32)[None, :]
    route_ids = jnp.arange(route_count, dtype=jnp.int32)
    before = (route_ids[None, :] < route_ids[:, None]).astype(jnp.bfloat16)
    earlier = jnp.dot(before, one_hot.astype(jnp.bfloat16), preferred_element_type=jnp.float32)
    position = jnp.sum(jnp.where(one_hot, earlier, 0.0), axis=1).astype(jnp.int32)
    slot_index = (flat_routes * capacity + position).reshape(tok_count, 2)
    slot_ids = jnp.arange(slot_count, dtype=jnp.int32)[:, None]
    first_hit = slot_ids == slot_index[:, 0][None, :]
    second_hit = slot_ids == slot_index[:, 1][None, :]
    pick = (first_hit | second_hit).astype(jnp.bfloat16)
    weigh = jnp.where(first_hit, gate_first[None, :], jnp.where(second_hit, 1.0 - gate_first[None, :], 0.0)).astype(
        jnp.bfloat16
    )
    pick = pick.reshape(expert_count, 1, capacity, tok_count)
    weigh = weigh.reshape(expert_count, 1, capacity, tok_count)
    blank = jnp.zeros_like(pick)
    gather_side = jnp.concatenate(
        [jnp.concatenate([pick, blank], axis=3), jnp.concatenate([blank, weigh], axis=3)], axis=1
    ).reshape(2 * slot_count, 2 * tok_count)
    return_side = jnp.concatenate(
        [jnp.concatenate([weigh, blank], axis=3), jnp.concatenate([blank, pick], axis=3)], axis=1
    ).reshape(2 * slot_count, 2 * tok_count)
    sources = jnp.concatenate([normed, cotangent], axis=0)
    sending = jnp.dot(gather_side, sources, preferred_element_type=jnp.float32).astype(jnp.bfloat16)
    arrived = lax.all_to_all(
        sending.reshape(expert_count, 2 * capacity, model_width), "expert", split_axis=0, concat_axis=0, tiled=True
    )
    expert_rows = arrived[:, :capacity].reshape(slot_count, model_width)
    grad_rows = arrived[:, capacity:].reshape(slot_count, model_width)
    pre_act = row_product(expert_rows, whole_up, 1)
    activated = gelu_value(pre_act).astype(jnp.bfloat16)
    expert_out = row_product(activated, whole_down, 0).astype(jnp.bfloat16)
    hidden_grad = row_product(grad_rows, whole_down, 1)
    pre_grad = (hidden_grad * gelu_slope(pre_act)).astype(jnp.bfloat16)
    normed_part = row_product(pre_grad, whole_up, 0).astype(jnp.bfloat16)
    leaving = jnp.concatenate(
        [expert_out.reshape(expert_count, capacity, model_width), normed_part.reshape(expert_count, capacity, model_width)],
        axis=1,
    )
    back = lax.all_to_all(leaving, "expert", split_axis=0, concat_axis=0, tiled=True)
    up_term = row_contract(pre_grad, expert_rows) * grad_scale
    down_term = row_contract(activated, grad_rows) * grad_scale
    parts = jnp.stack([up_term, down_term]).astype(jnp.bfloat16)
    parts = parts.reshape(2, cores, chips, -1, model_width).transpose(1, 2, 0, 3, 4)
    grad_pair = scatter_grads(parts, chips, cores)
    up_grad = grad_pair[0][None]
    down_grad = grad_pair[1][None]
    combined = row_contract(return_side, back.reshape(2 * slot_count, model_width))
    moe_output = combined[:tok_count].astype(jnp.bfloat16)
    normed_grad = combined[tok_count:]
    scaled = gain_rows * normed_grad
    token_grad = (
        inv_rms * scaled - x_float * inv_rms**3 * jnp.mean(x_float * scaled, axis=-1, keepdims=True)
    ).astype(jnp.bfloat16)
    return (moe_output, token_grad, up_grad, down_grad)


def solution(mesh):
    placed = (
        P(("dp", "expert"), None),
        P(("dp", "expert")),
        P(),
        P(("dp", "expert"), None),
        P(("dp", "expert")),
        P("expert", "dp", None),
        P("expert", "dp", None),
        P(("dp", "expert"), None),
    )
    return jax.shard_map(
        on_device,
        mesh=mesh,
        in_specs=placed,
        out_specs=(
            P(("dp", "expert"), None),
            P(("dp", "expert"), None),
            P("expert", "dp", None),
            P("expert", "dp", None),
        ),
        check_vma=False,
    )
```

```python
import math

import jax
import jax.numpy as jnp
from jax import lax
from jax.sharding import PartitionSpec as P

root_half = 0.7071067811865476
density = 0.3989422804014327


def gelu_value(values):
    return values * 0.5 * (1.0 + lax.erf(values * root_half))


def gelu_slope(values):
    return (
        0.5 * (1.0 + lax.erf(values * root_half))
        + values * jnp.exp(-0.5 * values * values) * density
    )


def row_product(left_side, right_side, right_axis):
    numbers = (((1,), (right_axis,)), ((), ()))
    return lax.dot_general(left_side, right_side, numbers, preferred_element_type=jnp.float32)


def row_contract(left_side, right_side):
    numbers = (((0,), (0,)), ((), ()))
    return lax.dot_general(left_side, right_side, numbers, preferred_element_type=jnp.float32)


def on_device(tokens, modality, modal_gains, routes, gate_share, up_weight, down_weight, cotangent):
    tok_count = tokens.shape[0]
    model_width = tokens.shape[1]
    expert_count = lax.axis_size("expert")
    replica_count = lax.axis_size("x") * lax.axis_size("core")
    capacity = 4 * tok_count // expert_count
    slot_count = expert_count * capacity
    route_count = 2 * tok_count
    grad_scale = 1.0 / math.sqrt(2 * tok_count * replica_count)
    shard = jnp.concatenate([up_weight, down_weight], axis=0)
    whole = lax.all_gather(lax.all_gather(shard, "x", axis=1, tiled=True), "core", axis=1, tiled=True)
    whole_up, whole_down = whole[0], whole[1]
    x_float = tokens.astype(jnp.float32)
    inv_rms = lax.rsqrt(jnp.mean(x_float * x_float, axis=-1, keepdims=True) + 1e-06)
    gain_rows = jnp.where(modality[:, None] == 1, modal_gains[1][None, :], modal_gains[0][None, :])
    normed = (x_float * inv_rms * gain_rows).astype(jnp.bfloat16)
    gate_first = gate_share.astype(jnp.float32) / 16.0
    flat_routes = routes.reshape(-1)
    one_hot = flat_routes[:, None] == jnp.arange(expert_count, dtype=jnp.int32)[None, :]
    route_ids = jnp.arange(route_count, dtype=jnp.int32)
    before = (route_ids[None, :] < route_ids[:, None]).astype(jnp.bfloat16)
    earlier = jnp.dot(before, one_hot.astype(jnp.bfloat16), preferred_element_type=jnp.float32)
    position = jnp.sum(jnp.where(one_hot, earlier, 0.0), axis=1).astype(jnp.int32)
    slot_index = (flat_routes * capacity + position).reshape(tok_count, 2)
    slot_ids = jnp.arange(slot_count, dtype=jnp.int32)[:, None]
    first_hit = slot_ids == slot_index[:, 0][None, :]
    second_hit = slot_ids == slot_index[:, 1][None, :]
    pick = (first_hit | second_hit).astype(jnp.bfloat16)
    weigh = jnp.where(first_hit, gate_first[None, :], jnp.where(second_hit, 1.0 - gate_first[None, :], 0.0)).astype(
        jnp.bfloat16
    )
    pick = pick.reshape(expert_count, 1, capacity, tok_count)
    weigh = weigh.reshape(expert_count, 1, capacity, tok_count)
    blank = jnp.zeros_like(pick)
    gather_side = jnp.concatenate(
        [jnp.concatenate([pick, blank], axis=3), jnp.concatenate([blank, weigh], axis=3)], axis=1
    ).reshape(2 * slot_count, 2 * tok_count)
    return_side = jnp.concatenate(
        [jnp.concatenate([weigh, blank], axis=3), jnp.concatenate([blank, pick], axis=3)], axis=1
    ).reshape(2 * slot_count, 2 * tok_count)
    sources = jnp.concatenate([normed, cotangent], axis=0)
    sending = jnp.dot(gather_side, sources, preferred_element_type=jnp.float32).astype(jnp.bfloat16)
    arrived = lax.all_to_all(
        sending.reshape(expert_count, 2 * capacity, model_width), "expert", split_axis=0, concat_axis=0, tiled=True
    )
    expert_rows = arrived[:, :capacity].reshape(slot_count, model_width)
    grad_rows = arrived[:, capacity:].reshape(slot_count, model_width)
    pre_act = row_product(expert_rows, whole_up, 1)
    activated = gelu_value(pre_act).astype(jnp.bfloat16)
    expert_out = row_product(activated, whole_down, 0).astype(jnp.bfloat16)
    hidden_grad = row_product(grad_rows, whole_down, 1)
    pre_grad = (hidden_grad * gelu_slope(pre_act)).astype(jnp.bfloat16)
    normed_part = row_product(pre_grad, whole_up, 0).astype(jnp.bfloat16)
    leaving = jnp.concatenate(
        [expert_out.reshape(expert_count, capacity, model_width), normed_part.reshape(expert_count, capacity, model_width)],
        axis=1,
    )
    back = lax.all_to_all(leaving, "expert", split_axis=0, concat_axis=0, tiled=True)
    up_term = row_contract(pre_grad, expert_rows) * grad_scale
    down_term = row_contract(activated, grad_rows) * grad_scale
    parts = jnp.stack([up_term, down_term], axis=1).astype(jnp.bfloat16)
    grad_pair = lax.psum_scatter(
        lax.psum_scatter(parts, "core", scatter_dimension=0, tiled=True), "x", scatter_dimension=0, tiled=True
    )
    up_grad = grad_pair[:, 0][None]
    down_grad = grad_pair[:, 1][None]
    combined = row_contract(return_side, back.reshape(2 * slot_count, model_width))
    moe_output = combined[:tok_count].astype(jnp.bfloat16)
    normed_grad = combined[tok_count:]
    scaled = gain_rows * normed_grad
    token_grad = (
        inv_rms * scaled - x_float * inv_rms**3 * jnp.mean(x_float * scaled, axis=-1, keepdims=True)
    ).astype(jnp.bfloat16)
    return (moe_output, token_grad, up_grad, down_grad)


def solution(mesh):
    dp_size, expert_size = mesh.devices.shape
    cores = 2
    mesh = jax.sharding.Mesh(mesh.devices.reshape(dp_size // cores, cores, expert_size), ("x", "core", "expert"))
    placed = (
        P(("x", "core", "expert"), None),
        P(("x", "core", "expert")),
        P(),
        P(("x", "core", "expert"), None),
        P(("x", "core", "expert")),
        P("expert", ("x", "core"), None),
        P("expert", ("x", "core"), None),
        P(("x", "core", "expert"), None),
    )
    return jax.shard_map(
        on_device,
        mesh=mesh,
        in_specs=placed,
        out_specs=(
            P(("x", "core", "expert"), None),
            P(("x", "core", "expert"), None),
            P("expert", ("x", "core"), None),
            P("expert", ("x", "core"), None),
        ),
        check_vma=False,
    )
```

```python
import math

import jax
import jax.numpy as jnp
from jax import lax
from jax.sharding import PartitionSpec as P

root_half = 0.7071067811865476
density = 0.3989422804014327


def gelu_value(values):
    return values * 0.5 * (1.0 + lax.erf(values * root_half))


def gelu_slope(values):
    return (
        0.5 * (1.0 + lax.erf(values * root_half))
        + values * jnp.exp(-0.5 * values * values) * density
    )


def row_product(left_side, right_side, right_axis):
    numbers = (((1,), (right_axis,)), ((), ()))
    return lax.dot_general(left_side, right_side, numbers, preferred_element_type=jnp.float32)


def row_contract(left_side, right_side):
    numbers = (((0,), (0,)), ((), ()))
    return lax.dot_general(left_side, right_side, numbers, preferred_element_type=jnp.float32)


def on_device(tokens, modality, modal_gains, routes, gate_share, up_weight, down_weight, cotangent):
    tok_count = tokens.shape[0]
    model_width = tokens.shape[1]
    expert_count = lax.axis_size("expert")
    replica_count = lax.axis_size("dp")
    capacity = 4 * tok_count // expert_count
    slot_count = expert_count * capacity
    route_count = 2 * tok_count
    grad_scale = 1.0 / math.sqrt(2 * tok_count * replica_count)
    whole = lax.all_gather(jnp.concatenate([up_weight, down_weight], axis=0), "dp", axis=1, tiled=True)
    whole_up, whole_down = whole[0], whole[1]
    x_float = tokens.astype(jnp.float32)
    inv_rms = lax.rsqrt(jnp.mean(x_float * x_float, axis=-1, keepdims=True) + 1e-06)
    gain_rows = jnp.where(modality[:, None] == 1, modal_gains[1][None, :], modal_gains[0][None, :])
    normed = (x_float * inv_rms * gain_rows).astype(jnp.bfloat16)
    gate_first = gate_share.astype(jnp.float32) / 16.0
    flat_routes = routes.reshape(-1)
    one_hot = flat_routes[:, None] == jnp.arange(expert_count, dtype=jnp.int32)[None, :]
    route_ids = jnp.arange(route_count, dtype=jnp.int32)
    before = (route_ids[None, :] < route_ids[:, None]).astype(jnp.bfloat16)
    earlier = jnp.dot(before, one_hot.astype(jnp.bfloat16), preferred_element_type=jnp.float32)
    position = jnp.sum(jnp.where(one_hot, earlier, 0.0), axis=1).astype(jnp.int32)
    slot_index = (flat_routes * capacity + position).reshape(tok_count, 2)
    slot_ids = jnp.arange(slot_count, dtype=jnp.int32)[:, None]
    first_hit = slot_ids == slot_index[:, 0][None, :]
    second_hit = slot_ids == slot_index[:, 1][None, :]
    pick = (first_hit | second_hit).astype(jnp.bfloat16)
    weigh = jnp.where(first_hit, gate_first[None, :], jnp.where(second_hit, 1.0 - gate_first[None, :], 0.0)).astype(
        jnp.bfloat16
    )
    pick = pick.reshape(expert_count, 1, capacity, tok_count)
    weigh = weigh.reshape(expert_count, 1, capacity, tok_count)
    blank = jnp.zeros_like(pick)
    gather_side = jnp.concatenate(
        [jnp.concatenate([pick, blank], axis=3), jnp.concatenate([blank, weigh], axis=3)], axis=1
    ).reshape(2 * slot_count, 2 * tok_count)
    return_side = jnp.concatenate(
        [jnp.concatenate([weigh, blank], axis=3), jnp.concatenate([blank, pick], axis=3)], axis=1
    ).reshape(2 * slot_count, 2 * tok_count)
    sources = jnp.concatenate([normed, cotangent], axis=0)
    sending = jnp.dot(gather_side, sources, preferred_element_type=jnp.float32).astype(jnp.bfloat16)
    arrived = lax.all_to_all(
        sending.reshape(expert_count, 2 * capacity, model_width), "expert", split_axis=0, concat_axis=0, tiled=True
    )
    expert_rows = arrived[:, :capacity].reshape(slot_count, model_width)
    grad_rows = arrived[:, capacity:].reshape(slot_count, model_width)
    pre_act = row_product(expert_rows, whole_up, 1)
    activated = gelu_value(pre_act).astype(jnp.bfloat16)
    expert_out = row_product(activated, whole_down, 0).astype(jnp.bfloat16)
    hidden_grad = row_product(grad_rows, whole_down, 1)
    pre_grad = (hidden_grad * gelu_slope(pre_act)).astype(jnp.bfloat16)
    normed_part = row_product(pre_grad, whole_up, 0).astype(jnp.bfloat16)
    leaving = jnp.concatenate(
        [expert_out.reshape(expert_count, capacity, model_width), normed_part.reshape(expert_count, capacity, model_width)],
        axis=1,
    )
    back = lax.all_to_all(leaving, "expert", split_axis=0, concat_axis=0, tiled=True)
    up_term = row_contract(pre_grad, expert_rows) * grad_scale
    down_term = row_contract(activated, grad_rows) * grad_scale
    parts = jnp.stack([up_term, down_term], axis=1).astype(jnp.bfloat16)
    grad_pair = lax.psum_scatter(parts, "dp", scatter_dimension=0, tiled=True)
    up_grad = grad_pair[:, 0][None]
    down_grad = grad_pair[:, 1][None]
    combined = row_contract(return_side, back.reshape(2 * slot_count, model_width))
    moe_output = combined[:tok_count].astype(jnp.bfloat16)
    normed_grad = combined[tok_count:]
    scaled = gain_rows * normed_grad
    token_grad = (
        inv_rms * scaled - x_float * inv_rms**3 * jnp.mean(x_float * scaled, axis=-1, keepdims=True)
    ).astype(jnp.bfloat16)
    return (moe_output, token_grad, up_grad, down_grad)


def solution(mesh):
    placed = (
        P(("dp", "expert"), None),
        P(("dp", "expert")),
        P(),
        P(("dp", "expert"), None),
        P(("dp", "expert")),
        P("expert", "dp", None),
        P("expert", "dp", None),
        P(("dp", "expert"), None),
    )
    return jax.shard_map(
        on_device,
        mesh=mesh,
        in_specs=placed,
        out_specs=(
            P(("dp", "expert"), None),
            P(("dp", "expert"), None),
            P("expert", "dp", None),
            P("expert", "dp", None),
        ),
        check_vma=False,
    )
```

```python
import math

import jax
import jax.numpy as jnp
from jax import lax
from jax.experimental import pallas as pl
from jax.experimental.pallas import tpu as pltpu
from jax.sharding import PartitionSpec as P

root_half = 0.7071067811865476
density = 0.3989422804014327


def gelu_value(values):
    return values * 0.5 * (1.0 + lax.erf(values * root_half))


def gelu_slope(values):
    return (
        0.5 * (1.0 + lax.erf(values * root_half))
        + values * jnp.exp(-0.5 * values * values) * density
    )


def row_product(left_side, right_side, right_axis):
    numbers = (((1,), (right_axis,)), ((), ()))
    return lax.dot_general(left_side, right_side, numbers, preferred_element_type=jnp.float32)


def row_contract(left_side, right_side):
    numbers = (((0,), (0,)), ((), ()))
    return lax.dot_general(left_side, right_side, numbers, preferred_element_type=jnp.float32)


def expert_body(x_ref, g_ref, up_ref, down_ref, out_ref, back_ref, grads_ref, out_acc, back_acc, *, scale):
    step = pl.program_id(0)

    @pl.when(step == 0)
    def _():
        out_acc[...] = jnp.zeros_like(out_acc)
        back_acc[...] = jnp.zeros_like(back_acc)

    x = x_ref[...]
    g = g_ref[...]
    up = up_ref[0]
    down = down_ref[0]
    pre_act = row_product(x, up, 1)
    activated = gelu_value(pre_act).astype(jnp.bfloat16)
    out_acc[...] += row_product(activated, down, 0)
    hidden_grad = row_product(g, down, 1)
    pre_grad = (hidden_grad * gelu_slope(pre_act)).astype(jnp.bfloat16)
    back_acc[...] += row_product(pre_grad, up, 0)
    grads_ref[0] = (row_contract(pre_grad, x) * scale).astype(jnp.bfloat16)
    grads_ref[1] = (row_contract(activated, g) * scale).astype(jnp.bfloat16)

    @pl.when(step == pl.num_programs(0) - 1)
    def _():
        out_ref[...] = out_acc[...].astype(jnp.bfloat16)
        back_ref[...] = back_acc[...].astype(jnp.bfloat16)


def expert_block(x_rows, g_rows, whole, scale, tile=512):
    rows, width = x_rows.shape
    hidden = whole.shape[1]
    flops = 12 * rows * hidden * width
    return pl.pallas_call(
        lambda *refs: expert_body(*refs, scale=scale),
        grid=(hidden // tile,),
        in_specs=[
            pl.BlockSpec((rows, width), lambda j: (0, 0)),
            pl.BlockSpec((rows, width), lambda j: (0, 0)),
            pl.BlockSpec((1, tile, width), lambda j: (0, j, 0)),
            pl.BlockSpec((1, tile, width), lambda j: (1, j, 0)),
        ],
        out_specs=[
            pl.BlockSpec((rows, width), lambda j: (0, 0)),
            pl.BlockSpec((rows, width), lambda j: (0, 0)),
            pl.BlockSpec((2, tile, width), lambda j: (0, j, 0)),
        ],
        out_shape=[
            jax.ShapeDtypeStruct((rows, width), jnp.bfloat16),
            jax.ShapeDtypeStruct((rows, width), jnp.bfloat16),
            jax.ShapeDtypeStruct((2, hidden, width), jnp.bfloat16),
        ],
        scratch_shapes=[pltpu.VMEM((rows, width), jnp.float32), pltpu.VMEM((rows, width), jnp.float32)],
        cost_estimate=pl.CostEstimate(
            flops=flops, transcendentals=2 * rows * hidden, bytes_accessed=2 * (4 * rows * width + 4 * hidden * width)
        ),
    )(x_rows, g_rows, whole, whole)


def on_device(tokens, modality, modal_gains, routes, gate_share, up_weight, down_weight, cotangent):
    tok_count = tokens.shape[0]
    model_width = tokens.shape[1]
    expert_count = lax.axis_size("expert")
    replica_count = lax.axis_size("dp")
    capacity = 4 * tok_count // expert_count
    slot_count = expert_count * capacity
    route_count = 2 * tok_count
    grad_scale = 1.0 / math.sqrt(2 * tok_count * replica_count)
    whole = lax.all_gather(jnp.concatenate([up_weight, down_weight], axis=0), "dp", axis=1, tiled=True)
    x_float = tokens.astype(jnp.float32)
    inv_rms = lax.rsqrt(jnp.mean(x_float * x_float, axis=-1, keepdims=True) + 1e-06)
    gain_rows = jnp.where(modality[:, None] == 1, modal_gains[1][None, :], modal_gains[0][None, :])
    normed = (x_float * inv_rms * gain_rows).astype(jnp.bfloat16)
    gate_first = gate_share.astype(jnp.float32) / 16.0
    flat_routes = routes.reshape(-1)
    one_hot = flat_routes[:, None] == jnp.arange(expert_count, dtype=jnp.int32)[None, :]
    route_ids = jnp.arange(route_count, dtype=jnp.int32)
    before = (route_ids[None, :] < route_ids[:, None]).astype(jnp.bfloat16)
    earlier = jnp.dot(before, one_hot.astype(jnp.bfloat16), preferred_element_type=jnp.float32)
    position = jnp.sum(jnp.where(one_hot, earlier, 0.0), axis=1).astype(jnp.int32)
    slot_index = (flat_routes * capacity + position).reshape(tok_count, 2)
    slot_ids = jnp.arange(slot_count, dtype=jnp.int32)[:, None]
    first_hit = slot_ids == slot_index[:, 0][None, :]
    second_hit = slot_ids == slot_index[:, 1][None, :]
    pick = (first_hit | second_hit).astype(jnp.bfloat16)
    weigh = jnp.where(first_hit, gate_first[None, :], jnp.where(second_hit, 1.0 - gate_first[None, :], 0.0)).astype(
        jnp.bfloat16
    )
    pick = pick.reshape(expert_count, 1, capacity, tok_count)
    weigh = weigh.reshape(expert_count, 1, capacity, tok_count)
    blank = jnp.zeros_like(pick)
    gather_side = jnp.concatenate(
        [jnp.concatenate([pick, blank], axis=3), jnp.concatenate([blank, weigh], axis=3)], axis=1
    ).reshape(2 * slot_count, 2 * tok_count)
    return_side = jnp.concatenate(
        [jnp.concatenate([weigh, blank], axis=3), jnp.concatenate([blank, pick], axis=3)], axis=1
    ).reshape(2 * slot_count, 2 * tok_count)
    sources = jnp.concatenate([normed, cotangent], axis=0)
    sending = jnp.dot(gather_side, sources, preferred_element_type=jnp.float32).astype(jnp.bfloat16)
    arrived = lax.all_to_all(
        sending.reshape(expert_count, 2 * capacity, model_width), "expert", split_axis=0, concat_axis=0, tiled=True
    )
    expert_rows = arrived[:, :capacity].reshape(slot_count, model_width)
    grad_rows = arrived[:, capacity:].reshape(slot_count, model_width)
    expert_out, normed_part, parts = expert_block(expert_rows, grad_rows, whole, grad_scale)
    leaving = jnp.concatenate(
        [expert_out.reshape(expert_count, capacity, model_width), normed_part.reshape(expert_count, capacity, model_width)],
        axis=1,
    )
    back = lax.all_to_all(leaving, "expert", split_axis=0, concat_axis=0, tiled=True)
    parts = parts.transpose(1, 0, 2)
    grad_pair = lax.psum_scatter(parts, "dp", scatter_dimension=0, tiled=True)
    up_grad = grad_pair[:, 0][None]
    down_grad = grad_pair[:, 1][None]
    combined = row_contract(return_side, back.reshape(2 * slot_count, model_width))
    moe_output = combined[:tok_count].astype(jnp.bfloat16)
    normed_grad = combined[tok_count:]
    scaled = gain_rows * normed_grad
    token_grad = (
        inv_rms * scaled - x_float * inv_rms**3 * jnp.mean(x_float * scaled, axis=-1, keepdims=True)
    ).astype(jnp.bfloat16)
    return (moe_output, token_grad, up_grad, down_grad)


def solution(mesh):
    placed = (
        P(("dp", "expert"), None),
        P(("dp", "expert")),
        P(),
        P(("dp", "expert"), None),
        P(("dp", "expert")),
        P("expert", "dp", None),
        P("expert", "dp", None),
        P(("dp", "expert"), None),
    )
    return jax.shard_map(
        on_device,
        mesh=mesh,
        in_specs=placed,
        out_specs=(
            P(("dp", "expert"), None),
            P(("dp", "expert"), None),
            P("expert", "dp", None),
            P("expert", "dp", None),
        ),
        check_vma=False,
    )
```

```python
import math

import jax
import jax.numpy as jnp
from jax import lax
from jax.experimental import pallas as pl
from jax.experimental.pallas import tpu as pltpu
from jax.sharding import PartitionSpec as P

root_half = 0.7071067811865476
density = 0.3989422804014327


def gelu_value(values):
    return values * 0.5 * (1.0 + lax.erf(values * root_half))


def gelu_slope(values):
    return (
        0.5 * (1.0 + lax.erf(values * root_half))
        + values * jnp.exp(-0.5 * values * values) * density
    )


def row_product(left_side, right_side, right_axis):
    numbers = (((1,), (right_axis,)), ((), ()))
    return lax.dot_general(left_side, right_side, numbers, preferred_element_type=jnp.float32)


def row_contract(left_side, right_side):
    numbers = (((0,), (0,)), ((), ()))
    return lax.dot_general(left_side, right_side, numbers, preferred_element_type=jnp.float32)


def expert_body(x_ref, g_ref, up_ref, down_ref, out_ref, back_ref, grads_ref, out_acc, back_acc, *, scale):
    step = pl.program_id(0)

    @pl.when(step == 0)
    def _():
        out_acc[...] = jnp.zeros_like(out_acc)
        back_acc[...] = jnp.zeros_like(back_acc)

    x = x_ref[...]
    g = g_ref[...]
    up = up_ref[0]
    down = down_ref[0]
    pre_act = row_product(x, up, 1)
    half_cdf = 0.5 * (1.0 + lax.erf(pre_act * root_half))
    activated = (pre_act * half_cdf).astype(jnp.bfloat16)
    out_acc[...] += row_product(activated, down, 0)
    hidden_grad = row_product(g, down, 1)
    slope = half_cdf + pre_act * jnp.exp(-0.5 * pre_act * pre_act) * density
    pre_grad = (hidden_grad * slope).astype(jnp.bfloat16)
    back_acc[...] += row_product(pre_grad, up, 0)
    grads_ref[0] = (row_contract(pre_grad, x) * scale).astype(jnp.bfloat16)
    grads_ref[1] = (row_contract(activated, g) * scale).astype(jnp.bfloat16)

    @pl.when(step == pl.num_programs(0) - 1)
    def _():
        out_ref[...] = out_acc[...].astype(jnp.bfloat16)
        back_ref[...] = back_acc[...].astype(jnp.bfloat16)


def expert_block(x_rows, g_rows, whole, scale, tile=512):
    rows, width = x_rows.shape
    hidden = whole.shape[1]
    flops = 12 * rows * hidden * width
    return pl.pallas_call(
        lambda *refs: expert_body(*refs, scale=scale),
        grid=(hidden // tile,),
        in_specs=[
            pl.BlockSpec((rows, width), lambda j: (0, 0)),
            pl.BlockSpec((rows, width), lambda j: (0, 0)),
            pl.BlockSpec((1, tile, width), lambda j: (0, j, 0)),
            pl.BlockSpec((1, tile, width), lambda j: (1, j, 0)),
        ],
        out_specs=[
            pl.BlockSpec((rows, width), lambda j: (0, 0)),
            pl.BlockSpec((rows, width), lambda j: (0, 0)),
            pl.BlockSpec((2, tile, width), lambda j: (0, j, 0)),
        ],
        out_shape=[
            jax.ShapeDtypeStruct((rows, width), jnp.bfloat16),
            jax.ShapeDtypeStruct((rows, width), jnp.bfloat16),
            jax.ShapeDtypeStruct((2, hidden, width), jnp.bfloat16),
        ],
        scratch_shapes=[pltpu.VMEM((rows, width), jnp.float32), pltpu.VMEM((rows, width), jnp.float32)],
        cost_estimate=pl.CostEstimate(
            flops=flops, transcendentals=2 * rows * hidden, bytes_accessed=2 * (4 * rows * width + 4 * hidden * width)
        ),
    )(x_rows, g_rows, whole, whole)


def copy_pieces_body(*refs, sources, targets):
    count = len(sources)
    sems = refs[-1]
    copies = []
    for i in range(count):
        (src, src_at), (dst, dst_at) = sources[i], targets[i]
        source = refs[src] if src_at is None else refs[src].at[src_at]
        target = refs[dst] if dst_at is None else refs[dst].at[dst_at]
        copies.append(pltpu.make_async_copy(source, target, sems.at[i]))
    for c in copies:
        c.start()
    for c in copies:
        c.wait()


def copy_pieces(arrays, out_shapes, sources, targets):
    anywhere = pl.BlockSpec(memory_space=pl.ANY)
    return pl.pallas_call(
        lambda *refs: copy_pieces_body(*refs, sources=sources, targets=targets),
        in_specs=[anywhere] * len(arrays),
        out_specs=[anywhere] * len(out_shapes),
        out_shape=out_shapes,
        scratch_shapes=[pltpu.SemaphoreType.DMA((len(sources),))],
    )(*arrays)


def on_device(tokens, modality, modal_gains, routes, gate_share, up_weight, down_weight, cotangent):
    tok_count = tokens.shape[0]
    model_width = tokens.shape[1]
    expert_count = lax.axis_size("expert")
    replica_count = lax.axis_size("dp")
    capacity = 4 * tok_count // expert_count
    slot_count = expert_count * capacity
    route_count = 2 * tok_count
    grad_scale = 1.0 / math.sqrt(2 * tok_count * replica_count)
    both = jax.ShapeDtypeStruct((2,) + up_weight.shape[1:], up_weight.dtype)
    (shard,) = copy_pieces([up_weight, down_weight], [both], [(0, 0), (1, 0)], [(2, 0), (2, 1)])
    whole = lax.all_gather(shard, "dp", axis=1, tiled=True)
    x_float = tokens.astype(jnp.float32)
    inv_rms = lax.rsqrt(jnp.mean(x_float * x_float, axis=-1, keepdims=True) + 1e-06)
    gain_rows = jnp.where(modality[:, None] == 1, modal_gains[1][None, :], modal_gains[0][None, :])
    normed = (x_float * inv_rms * gain_rows).astype(jnp.bfloat16)
    gate_first = gate_share.astype(jnp.float32) / 16.0
    flat_routes = routes.reshape(-1)
    one_hot = flat_routes[:, None] == jnp.arange(expert_count, dtype=jnp.int32)[None, :]
    route_ids = jnp.arange(route_count, dtype=jnp.int32)
    before = (route_ids[None, :] < route_ids[:, None]).astype(jnp.bfloat16)
    earlier = jnp.dot(before, one_hot.astype(jnp.bfloat16), preferred_element_type=jnp.float32)
    position = jnp.sum(jnp.where(one_hot, earlier, 0.0), axis=1).astype(jnp.int32)
    slot_index = (flat_routes * capacity + position).reshape(tok_count, 2)
    slot_ids = jnp.arange(slot_count, dtype=jnp.int32)[:, None]
    first_hit = slot_ids == slot_index[:, 0][None, :]
    second_hit = slot_ids == slot_index[:, 1][None, :]
    pick = (first_hit | second_hit).astype(jnp.bfloat16)
    weigh = jnp.where(first_hit, gate_first[None, :], jnp.where(second_hit, 1.0 - gate_first[None, :], 0.0)).astype(
        jnp.bfloat16
    )
    pick = pick.reshape(expert_count, 1, capacity, tok_count)
    weigh = weigh.reshape(expert_count, 1, capacity, tok_count)
    blank = jnp.zeros_like(pick)
    gather_side = jnp.concatenate(
        [jnp.concatenate([pick, blank], axis=3), jnp.concatenate([blank, weigh], axis=3)], axis=1
    ).reshape(2 * slot_count, 2 * tok_count)
    return_side = jnp.concatenate(
        [jnp.concatenate([weigh, blank], axis=3), jnp.concatenate([blank, pick], axis=3)], axis=1
    ).reshape(2 * slot_count, 2 * tok_count)
    sources = jnp.concatenate([normed, cotangent], axis=0)
    sending = jnp.dot(gather_side, sources, preferred_element_type=jnp.float32).astype(jnp.bfloat16)
    arrived = lax.all_to_all(
        sending.reshape(expert_count, 2 * capacity, model_width), "expert", split_axis=0, concat_axis=0, tiled=True
    )
    expert_rows = arrived[:, :capacity].reshape(slot_count, model_width)
    grad_rows = arrived[:, capacity:].reshape(slot_count, model_width)
    expert_out, normed_part, parts = expert_block(expert_rows, grad_rows, whole, grad_scale)
    leaving = jnp.concatenate(
        [expert_out.reshape(expert_count, capacity, model_width), normed_part.reshape(expert_count, capacity, model_width)],
        axis=1,
    )
    back = lax.all_to_all(leaving, "expert", split_axis=0, concat_axis=0, tiled=True)
    grad_pair = lax.psum_scatter(parts, "dp", scatter_dimension=1, tiled=True)
    one = jax.ShapeDtypeStruct((1,) + grad_pair.shape[1:], grad_pair.dtype)
    up_grad, down_grad = copy_pieces([grad_pair], [one, one], [(0, 0), (0, 1)], [(1, 0), (2, 0)])
    combined = row_contract(return_side, back.reshape(2 * slot_count, model_width))
    moe_output = combined[:tok_count].astype(jnp.bfloat16)
    normed_grad = combined[tok_count:]
    scaled = gain_rows * normed_grad
    token_grad = (
        inv_rms * scaled - x_float * inv_rms**3 * jnp.mean(x_float * scaled, axis=-1, keepdims=True)
    ).astype(jnp.bfloat16)
    return (moe_output, token_grad, up_grad, down_grad)


def solution(mesh):
    placed = (
        P(("dp", "expert"), None),
        P(("dp", "expert")),
        P(),
        P(("dp", "expert"), None),
        P(("dp", "expert")),
        P("expert", "dp", None),
        P("expert", "dp", None),
        P(("dp", "expert"), None),
    )
    return jax.shard_map(
        on_device,
        mesh=mesh,
        in_specs=placed,
        out_specs=(
            P(("dp", "expert"), None),
            P(("dp", "expert"), None),
            P("expert", "dp", None),
            P("expert", "dp", None),
        ),
        check_vma=False,
    )
```

```python
import math

import jax
import jax.numpy as jnp
from jax import lax
from jax.experimental import pallas as pl
from jax.experimental.pallas import tpu as pltpu
from jax.sharding import PartitionSpec as P

root_half = 0.7071067811865476
density = 0.3989422804014327


def gelu_value(values):
    return values * 0.5 * (1.0 + lax.erf(values * root_half))


def gelu_slope(values):
    return (
        0.5 * (1.0 + lax.erf(values * root_half))
        + values * jnp.exp(-0.5 * values * values) * density
    )


def row_product(left_side, right_side, right_axis):
    numbers = (((1,), (right_axis,)), ((), ()))
    return lax.dot_general(left_side, right_side, numbers, preferred_element_type=jnp.float32)


def row_contract(left_side, right_side):
    numbers = (((0,), (0,)), ((), ()))
    return lax.dot_general(left_side, right_side, numbers, preferred_element_type=jnp.float32)


def expert_body(x_ref, g_ref, up_ref, down_ref, leaving_ref, grads_ref, out_acc, back_acc, *, scale):
    step = pl.program_id(0)
    @pl.when(step == 0)
    def _():
        out_acc[...] = jnp.zeros_like(out_acc)
        back_acc[...] = jnp.zeros_like(back_acc)
    sources, capacity, width = x_ref.shape
    x = x_ref[...].reshape(sources * capacity, width)
    g = g_ref[...].reshape(sources * capacity, width)
    up = up_ref[0]
    down = down_ref[0]
    pre_act = row_product(x, up, 1)
    half_cdf = 0.5 * (1.0 + lax.erf(pre_act * root_half))
    activated = (pre_act * half_cdf).astype(jnp.bfloat16)
    out_acc[...] += row_product(activated, down, 0)
    hidden_grad = row_product(g, down, 1)
    slope = half_cdf + pre_act * jnp.exp(-0.5 * pre_act * pre_act) * density
    pre_grad = (hidden_grad * slope).astype(jnp.bfloat16)
    back_acc[...] += row_product(pre_grad, up, 0)
    grads_ref[0] = (row_contract(pre_grad, x) * scale).astype(jnp.bfloat16)
    grads_ref[1] = (row_contract(activated, g) * scale).astype(jnp.bfloat16)
    @pl.when(step == pl.num_programs(0) - 1)
    def _():
        leaving_ref[:, :capacity, :] = out_acc[...].astype(jnp.bfloat16).reshape(sources, capacity, width)
        leaving_ref[:, capacity:, :] = back_acc[...].astype(jnp.bfloat16).reshape(sources, capacity, width)

def expert_block(arrived, whole, scale, tile=1024):
    sources, both, width = arrived.shape
    capacity = both // 2
    rows = sources * capacity
    hidden = whole.shape[1]
    return pl.pallas_call(
        lambda *refs: expert_body(*refs, scale=scale),
        grid=(hidden // tile,),
        in_specs=[
            pl.BlockSpec((sources, capacity, width), lambda j: (0, 0, 0)),
            pl.BlockSpec((sources, capacity, width), lambda j: (0, 1, 0)),
            pl.BlockSpec((1, tile, width), lambda j: (0, j, 0)),
            pl.BlockSpec((1, tile, width), lambda j: (1, j, 0)),
        ],
        out_specs=[
            pl.BlockSpec((sources, both, width), lambda j: (0, 0, 0)),
            pl.BlockSpec((2, tile, width), lambda j: (0, j, 0)),
        ],
        out_shape=[
            jax.ShapeDtypeStruct((sources, both, width), jnp.bfloat16),
            jax.ShapeDtypeStruct((2, hidden, width), jnp.bfloat16),
        ],
        scratch_shapes=[pltpu.VMEM((rows, width), jnp.float32), pltpu.VMEM((rows, width), jnp.float32)],
        cost_estimate=pl.CostEstimate(flops=12 * rows * hidden * width, transcendentals=2 * rows * hidden,
                                      bytes_accessed=2 * (4 * rows * width + 4 * hidden * width)),
    )(arrived, arrived, whole, whole)


def on_device(tokens, modality, modal_gains, routes, gate_share, up_weight, down_weight, cotangent):
    tok_count = tokens.shape[0]
    model_width = tokens.shape[1]
    expert_count = lax.axis_size("expert")
    replica_count = lax.axis_size("dp")
    capacity = 4 * tok_count // expert_count
    slot_count = expert_count * capacity
    route_count = 2 * tok_count
    grad_scale = 1.0 / math.sqrt(2 * tok_count * replica_count)
    whole = lax.all_gather(jnp.concatenate([up_weight, down_weight], axis=0), "dp", axis=1, tiled=True)
    x_float = tokens.astype(jnp.float32)
    inv_rms = lax.rsqrt(jnp.mean(x_float * x_float, axis=-1, keepdims=True) + 1e-06)
    gain_rows = jnp.where(modality[:, None] == 1, modal_gains[1][None, :], modal_gains[0][None, :])
    normed = (x_float * inv_rms * gain_rows).astype(jnp.bfloat16)
    gate_first = gate_share.astype(jnp.float32) / 16.0
    flat_routes = routes.reshape(-1)
    one_hot = flat_routes[:, None] == jnp.arange(expert_count, dtype=jnp.int32)[None, :]
    route_ids = jnp.arange(route_count, dtype=jnp.int32)
    before = (route_ids[None, :] < route_ids[:, None]).astype(jnp.bfloat16)
    earlier = jnp.dot(before, one_hot.astype(jnp.bfloat16), preferred_element_type=jnp.float32)
    position = jnp.sum(jnp.where(one_hot, earlier, 0.0), axis=1).astype(jnp.int32)
    slot_index = (flat_routes * capacity + position).reshape(tok_count, 2)
    slot_ids = jnp.arange(slot_count, dtype=jnp.int32)[:, None]
    first_hit = slot_ids == slot_index[:, 0][None, :]
    second_hit = slot_ids == slot_index[:, 1][None, :]
    pick = (first_hit | second_hit).astype(jnp.bfloat16)
    weigh = jnp.where(first_hit, gate_first[None, :], jnp.where(second_hit, 1.0 - gate_first[None, :], 0.0)).astype(
        jnp.bfloat16
    )
    pick = pick.reshape(expert_count, 1, capacity, tok_count)
    weigh = weigh.reshape(expert_count, 1, capacity, tok_count)
    blank = jnp.zeros_like(pick)
    gather_side = jnp.concatenate(
        [jnp.concatenate([pick, blank], axis=3), jnp.concatenate([blank, weigh], axis=3)], axis=1
    ).reshape(2 * slot_count, 2 * tok_count)
    return_side = jnp.concatenate(
        [jnp.concatenate([weigh, blank], axis=3), jnp.concatenate([blank, pick], axis=3)], axis=1
    ).reshape(2 * slot_count, 2 * tok_count)
    sources = jnp.concatenate([normed, cotangent], axis=0)
    sending = jnp.dot(gather_side, sources, preferred_element_type=jnp.float32).astype(jnp.bfloat16)
    arrived = lax.all_to_all(
        sending.reshape(expert_count, 2 * capacity, model_width), "expert", split_axis=0, concat_axis=0, tiled=True
    )
    leaving, parts = expert_block(arrived, whole, grad_scale)
    back = lax.all_to_all(leaving, "expert", split_axis=0, concat_axis=0, tiled=True)
    parts = parts.transpose(1, 0, 2)
    grad_pair = lax.psum_scatter(parts, "dp", scatter_dimension=0, tiled=True)
    up_grad = grad_pair[:, 0][None]
    down_grad = grad_pair[:, 1][None]
    combined = row_contract(return_side, back.reshape(2 * slot_count, model_width))
    moe_output = combined[:tok_count].astype(jnp.bfloat16)
    normed_grad = combined[tok_count:]
    scaled = gain_rows * normed_grad
    token_grad = (
        inv_rms * scaled - x_float * inv_rms**3 * jnp.mean(x_float * scaled, axis=-1, keepdims=True)
    ).astype(jnp.bfloat16)
    return (moe_output, token_grad, up_grad, down_grad)


def solution(mesh):
    placed = (
        P(("dp", "expert"), None),
        P(("dp", "expert")),
        P(),
        P(("dp", "expert"), None),
        P(("dp", "expert")),
        P("expert", "dp", None),
        P("expert", "dp", None),
        P(("dp", "expert"), None),
    )
    return jax.shard_map(
        on_device,
        mesh=mesh,
        in_specs=placed,
        out_specs=(
            P(("dp", "expert"), None),
            P(("dp", "expert"), None),
            P("expert", "dp", None),
            P("expert", "dp", None),
        ),
        check_vma=False,
    )
```

```python
import math

import jax
import jax.numpy as jnp
from jax import lax
from jax.experimental import pallas as pl
from jax.experimental.pallas import tpu as pltpu
from jax.sharding import PartitionSpec as P

root_half = 0.7071067811865476
density = 0.3989422804014327


def gelu_value(values):
    return values * 0.5 * (1.0 + lax.erf(values * root_half))


def gelu_slope(values):
    return (
        0.5 * (1.0 + lax.erf(values * root_half))
        + values * jnp.exp(-0.5 * values * values) * density
    )


def row_product(left_side, right_side, right_axis):
    numbers = (((1,), (right_axis,)), ((), ()))
    return lax.dot_general(left_side, right_side, numbers, preferred_element_type=jnp.float32)


def row_contract(left_side, right_side):
    numbers = (((0,), (0,)), ((), ()))
    return lax.dot_general(left_side, right_side, numbers, preferred_element_type=jnp.float32)


def expert_body(arrived_ref, up_ref, down_ref, leaving_ref, grads_ref, out_acc, back_acc, *, scale):
    step = pl.program_id(0)
    @pl.when(step == 0)
    def _():
        out_acc[...] = jnp.zeros_like(out_acc)
        back_acc[...] = jnp.zeros_like(back_acc)
    sources, both, width = arrived_ref.shape
    capacity = both // 2
    x = arrived_ref[:, :capacity, :].reshape(sources * capacity, width)
    g = arrived_ref[:, capacity:, :].reshape(sources * capacity, width)
    up = up_ref[0]
    down = down_ref[0]
    pre_act = row_product(x, up, 1)
    half_cdf = 0.5 * (1.0 + lax.erf(pre_act * root_half))
    activated = (pre_act * half_cdf).astype(jnp.bfloat16)
    out_acc[...] += row_product(activated, down, 0)
    hidden_grad = row_product(g, down, 1)
    slope = half_cdf + pre_act * jnp.exp(-0.5 * pre_act * pre_act) * density
    pre_grad = (hidden_grad * slope).astype(jnp.bfloat16)
    back_acc[...] += row_product(pre_grad, up, 0)
    grads_ref[0] = (row_contract(pre_grad, x) * scale).astype(jnp.bfloat16)
    grads_ref[1] = (row_contract(activated, g) * scale).astype(jnp.bfloat16)
    @pl.when(step == pl.num_programs(0) - 1)
    def _():
        leaving_ref[:, :capacity, :] = out_acc[...].astype(jnp.bfloat16).reshape(sources, capacity, width)
        leaving_ref[:, capacity:, :] = back_acc[...].astype(jnp.bfloat16).reshape(sources, capacity, width)

def expert_block(arrived, whole, scale, tile=512):
    sources, both, width = arrived.shape
    capacity = both // 2
    rows = sources * capacity
    hidden = whole.shape[1]
    return pl.pallas_call(
        lambda *refs: expert_body(*refs, scale=scale),
        grid=(hidden // tile,),
        in_specs=[
            pl.BlockSpec((sources, both, width), lambda j: (0, 0, 0)),
            pl.BlockSpec((1, tile, width), lambda j: (0, j, 0)),
            pl.BlockSpec((1, tile, width), lambda j: (1, j, 0)),
        ],
        out_specs=[
            pl.BlockSpec((sources, both, width), lambda j: (0, 0, 0)),
            pl.BlockSpec((2, tile, width), lambda j: (0, j, 0)),
        ],
        out_shape=[
            jax.ShapeDtypeStruct((sources, both, width), jnp.bfloat16),
            jax.ShapeDtypeStruct((2, hidden, width), jnp.bfloat16),
        ],
        scratch_shapes=[pltpu.VMEM((rows, width), jnp.float32), pltpu.VMEM((rows, width), jnp.float32)],
        cost_estimate=pl.CostEstimate(flops=12 * rows * hidden * width, transcendentals=2 * rows * hidden,
                                      bytes_accessed=2 * (4 * rows * width + 4 * hidden * width)),
    )(arrived, whole, whole)


def prologue_body(tokens_ref, cot_ref, modality_ref, gains_ref, routes_ref, share_ref, send_ref, back_side_ref,
                  *, experts, capacity):
    tok_count, width = tokens_ref.shape
    slots = experts * capacity
    x = tokens_ref[...].astype(jnp.float32)
    inv_rms = lax.rsqrt(jnp.mean(x * x, axis=-1, keepdims=True) + 1e-06)
    gains = gains_ref[...]
    gain_rows = jnp.where(modality_ref[...] == 1, gains[1:2, :], gains[0:1, :])
    normed = (x * inv_rms * gain_rows).astype(jnp.bfloat16)
    routes = routes_ref[...]
    first = routes[0:1, :]
    second = routes[1:2, :]
    expert_ids = lax.broadcasted_iota(jnp.int32, (experts, tok_count), 0)
    hot_first = (first == expert_ids).astype(jnp.float32)
    hot_second = (second == expert_ids).astype(jnp.float32)
    rows = lax.broadcasted_iota(jnp.int32, (tok_count, tok_count), 0)
    cols = lax.broadcasted_iota(jnp.int32, (tok_count, tok_count), 1)
    after = (rows < cols).astype(jnp.bfloat16)
    earlier = jnp.dot((hot_first + hot_second).astype(jnp.bfloat16), after, preferred_element_type=jnp.float32)
    rank_first = jnp.sum(earlier * hot_first, axis=0, keepdims=True).astype(jnp.int32)
    rank_second = jnp.sum(earlier * hot_second, axis=0, keepdims=True).astype(jnp.int32)
    slot_ids = lax.broadcasted_iota(jnp.int32, (slots, tok_count), 0)
    hit_first = slot_ids == first * capacity + rank_first
    hit_second = slot_ids == second * capacity + rank_second
    gate_first = share_ref[...].astype(jnp.float32) / 16.0
    pick = (hit_first | hit_second).astype(jnp.bfloat16)
    weigh = jnp.where(hit_first, gate_first, jnp.where(hit_second, 1.0 - gate_first, 0.0)).astype(jnp.bfloat16)
    token_rows = jnp.dot(pick, normed, preferred_element_type=jnp.float32).astype(jnp.bfloat16)
    grad_rows = jnp.dot(weigh, cot_ref[...], preferred_element_type=jnp.float32).astype(jnp.bfloat16)
    send_ref[:, :capacity, :] = token_rows.reshape(experts, capacity, width)
    send_ref[:, capacity:, :] = grad_rows.reshape(experts, capacity, width)
    blank = jnp.zeros_like(pick)
    back_side_ref[:, :capacity, :] = jnp.concatenate([weigh, blank], axis=1).reshape(experts, capacity, 2 * tok_count)
    back_side_ref[:, capacity:, :] = jnp.concatenate([blank, pick], axis=1).reshape(experts, capacity, 2 * tok_count)


def prologue(tokens, cotangent, modality, modal_gains, routes, gate_share, experts, capacity):
    tok_count, width = tokens.shape
    whole = lambda shape: pl.BlockSpec(shape, lambda: (0,) * len(shape))
    return pl.pallas_call(
        lambda *refs: prologue_body(*refs, experts=experts, capacity=capacity),
        in_specs=[whole((tok_count, width)), whole((tok_count, width)), whole((tok_count, 1)), whole((2, width)),
                  whole((2, tok_count)), whole((1, tok_count))],
        out_specs=[whole((experts, 2 * capacity, width)), whole((experts, 2 * capacity, 2 * tok_count))],
        out_shape=[
            jax.ShapeDtypeStruct((experts, 2 * capacity, width), jnp.bfloat16),
            jax.ShapeDtypeStruct((experts, 2 * capacity, 2 * tok_count), jnp.bfloat16),
        ],
    )(tokens, cotangent, modality.reshape(tok_count, 1), modal_gains, routes.T, gate_share.reshape(1, tok_count))


def on_device(tokens, modality, modal_gains, routes, gate_share, up_weight, down_weight, cotangent):
    tok_count = tokens.shape[0]
    model_width = tokens.shape[1]
    expert_count = lax.axis_size("expert")
    replica_count = lax.axis_size("dp")
    capacity = 4 * tok_count // expert_count
    slot_count = expert_count * capacity
    route_count = 2 * tok_count
    grad_scale = 1.0 / math.sqrt(2 * tok_count * replica_count)
    whole = lax.all_gather(jnp.concatenate([up_weight, down_weight], axis=0), "dp", axis=1, tiled=True)
    sending, return_side = prologue(tokens, cotangent, modality, modal_gains, routes, gate_share, expert_count, capacity)
    arrived = lax.all_to_all(sending, "expert", split_axis=0, concat_axis=0, tiled=True)
    leaving, parts = expert_block(arrived, whole, grad_scale)
    back = lax.all_to_all(leaving, "expert", split_axis=0, concat_axis=0, tiled=True)
    parts = parts.transpose(1, 0, 2)
    grad_pair = lax.psum_scatter(parts, "dp", scatter_dimension=0, tiled=True)
    up_grad = grad_pair[:, 0][None]
    down_grad = grad_pair[:, 1][None]
    combined = row_contract(return_side.reshape(2 * slot_count, 2 * tok_count), back.reshape(2 * slot_count, model_width))
    x_float = tokens.astype(jnp.float32)
    inv_rms = lax.rsqrt(jnp.mean(x_float * x_float, axis=-1, keepdims=True) + 1e-06)
    gain_rows = jnp.where(modality[:, None] == 1, modal_gains[1][None, :], modal_gains[0][None, :])
    moe_output = combined[:tok_count].astype(jnp.bfloat16)
    normed_grad = combined[tok_count:]
    scaled = gain_rows * normed_grad
    token_grad = (
        inv_rms * scaled - x_float * inv_rms**3 * jnp.mean(x_float * scaled, axis=-1, keepdims=True)
    ).astype(jnp.bfloat16)
    return (moe_output, token_grad, up_grad, down_grad)


def solution(mesh):
    placed = (
        P(("dp", "expert"), None),
        P(("dp", "expert")),
        P(),
        P(("dp", "expert"), None),
        P(("dp", "expert")),
        P("expert", "dp", None),
        P("expert", "dp", None),
        P(("dp", "expert"), None),
    )
    return jax.shard_map(
        on_device,
        mesh=mesh,
        in_specs=placed,
        out_specs=(
            P(("dp", "expert"), None),
            P(("dp", "expert"), None),
            P("expert", "dp", None),
            P("expert", "dp", None),
        ),
        check_vma=False,
    )
```

```python
import math

import jax
import jax.numpy as jnp
from jax import lax
from jax.experimental import pallas as pl
from jax.experimental.pallas import tpu as pltpu
from jax.sharding import PartitionSpec as P

root_half = 0.7071067811865476
density = 0.3989422804014327


def gelu_value(values):
    return values * 0.5 * (1.0 + lax.erf(values * root_half))


def gelu_slope(values):
    return (
        0.5 * (1.0 + lax.erf(values * root_half))
        + values * jnp.exp(-0.5 * values * values) * density
    )


def row_product(left_side, right_side, right_axis):
    numbers = (((1,), (right_axis,)), ((), ()))
    return lax.dot_general(left_side, right_side, numbers, preferred_element_type=jnp.float32)


def row_contract(left_side, right_side):
    numbers = (((0,), (0,)), ((), ()))
    return lax.dot_general(left_side, right_side, numbers, preferred_element_type=jnp.float32)


def expert_body(arrived_ref, up_ref, down_ref, leaving_ref, grads_ref, out_acc, back_acc, *, scale):
    step = pl.program_id(0)
    @pl.when(step == 0)
    def _():
        out_acc[...] = jnp.zeros_like(out_acc)
        back_acc[...] = jnp.zeros_like(back_acc)
    sources, both, width = arrived_ref.shape
    capacity = both // 2
    x = arrived_ref[:, :capacity, :].reshape(sources * capacity, width)
    g = arrived_ref[:, capacity:, :].reshape(sources * capacity, width)
    up = up_ref[0]
    down = down_ref[0]
    pre_act = row_product(x, up, 1)
    half_cdf = 0.5 * (1.0 + lax.erf(pre_act * root_half))
    activated = (pre_act * half_cdf).astype(jnp.bfloat16)
    out_acc[...] += row_product(activated, down, 0)
    hidden_grad = row_product(g, down, 1)
    slope = half_cdf + pre_act * jnp.exp(-0.5 * pre_act * pre_act) * density
    pre_grad = (hidden_grad * slope).astype(jnp.bfloat16)
    back_acc[...] += row_product(pre_grad, up, 0)
    grads_ref[0] = (row_contract(pre_grad, x) * scale).astype(jnp.bfloat16)
    grads_ref[1] = (row_contract(activated, g) * scale).astype(jnp.bfloat16)
    @pl.when(step == pl.num_programs(0) - 1)
    def _():
        leaving_ref[:, :capacity, :] = out_acc[...].astype(jnp.bfloat16).reshape(sources, capacity, width)
        leaving_ref[:, capacity:, :] = back_acc[...].astype(jnp.bfloat16).reshape(sources, capacity, width)

def expert_block(arrived, whole, scale, tile=512):
    sources, both, width = arrived.shape
    capacity = both // 2
    rows = sources * capacity
    hidden = whole.shape[1]
    return pl.pallas_call(
        lambda *refs: expert_body(*refs, scale=scale),
        grid=(hidden // tile,),
        in_specs=[
            pl.BlockSpec((sources, both, width), lambda j: (0, 0, 0)),
            pl.BlockSpec((1, tile, width), lambda j: (0, j, 0)),
            pl.BlockSpec((1, tile, width), lambda j: (1, j, 0)),
        ],
        out_specs=[
            pl.BlockSpec((sources, both, width), lambda j: (0, 0, 0)),
            pl.BlockSpec((2, tile, width), lambda j: (0, j, 0)),
        ],
        out_shape=[
            jax.ShapeDtypeStruct((sources, both, width), jnp.bfloat16),
            jax.ShapeDtypeStruct((2, hidden, width), jnp.bfloat16),
        ],
        scratch_shapes=[pltpu.VMEM((rows, width), jnp.float32), pltpu.VMEM((rows, width), jnp.float32)],
        cost_estimate=pl.CostEstimate(flops=12 * rows * hidden * width, transcendentals=2 * rows * hidden,
                                      bytes_accessed=2 * (4 * rows * width + 4 * hidden * width)),
    )(arrived, whole, whole)


def prologue_body(tokens_ref, cot_ref, modality_ref, gains_ref, routes_ref, share_ref, up_ref, down_ref,
                  send_ref, back_side_ref, shard_ref, *, experts, capacity):
    shard_ref[0] = up_ref[0]
    shard_ref[1] = down_ref[0]
    tok_count, width = tokens_ref.shape
    slots = experts * capacity
    x = tokens_ref[...].astype(jnp.float32)
    inv_rms = lax.rsqrt(jnp.mean(x * x, axis=-1, keepdims=True) + 1e-06)
    gains = gains_ref[...]
    gain_rows = jnp.where(modality_ref[...] == 1, gains[1:2, :], gains[0:1, :])
    normed = (x * inv_rms * gain_rows).astype(jnp.bfloat16)
    routes = routes_ref[...]
    first = routes[0:1, :]
    second = routes[1:2, :]
    expert_ids = lax.broadcasted_iota(jnp.int32, (experts, tok_count), 0)
    hot_first = (first == expert_ids).astype(jnp.float32)
    hot_second = (second == expert_ids).astype(jnp.float32)
    rows = lax.broadcasted_iota(jnp.int32, (tok_count, tok_count), 0)
    cols = lax.broadcasted_iota(jnp.int32, (tok_count, tok_count), 1)
    after = (rows < cols).astype(jnp.bfloat16)
    earlier = jnp.dot((hot_first + hot_second).astype(jnp.bfloat16), after, preferred_element_type=jnp.float32)
    rank_first = jnp.sum(earlier * hot_first, axis=0, keepdims=True).astype(jnp.int32)
    rank_second = jnp.sum(earlier * hot_second, axis=0, keepdims=True).astype(jnp.int32)
    slot_ids = lax.broadcasted_iota(jnp.int32, (slots, tok_count), 0)
    hit_first = slot_ids == first * capacity + rank_first
    hit_second = slot_ids == second * capacity + rank_second
    gate_first = share_ref[...].astype(jnp.float32) / 16.0
    pick = (hit_first | hit_second).astype(jnp.bfloat16)
    weigh = jnp.where(hit_first, gate_first, jnp.where(hit_second, 1.0 - gate_first, 0.0)).astype(jnp.bfloat16)
    token_rows = jnp.dot(pick, normed, preferred_element_type=jnp.float32).astype(jnp.bfloat16)
    grad_rows = jnp.dot(weigh, cot_ref[...], preferred_element_type=jnp.float32).astype(jnp.bfloat16)
    send_ref[:, :capacity, :] = token_rows.reshape(experts, capacity, width)
    send_ref[:, capacity:, :] = grad_rows.reshape(experts, capacity, width)
    blank = jnp.zeros_like(pick)
    back_side_ref[:, :capacity, :] = jnp.concatenate([weigh, blank], axis=1).reshape(experts, capacity, 2 * tok_count)
    back_side_ref[:, capacity:, :] = jnp.concatenate([blank, pick], axis=1).reshape(experts, capacity, 2 * tok_count)


def prologue(tokens, cotangent, modality, modal_gains, routes, gate_share, up_weight, down_weight, experts, capacity):
    tok_count, width = tokens.shape
    whole = lambda shape: pl.BlockSpec(shape, lambda: (0,) * len(shape))
    return pl.pallas_call(
        lambda *refs: prologue_body(*refs, experts=experts, capacity=capacity),
        in_specs=[whole((tok_count, width)), whole((tok_count, width)), whole((tok_count, 1)), whole((2, width)),
                  whole((2, tok_count)), whole((1, tok_count)), whole(up_weight.shape), whole(down_weight.shape)],
        out_specs=[whole((experts, 2 * capacity, width)), whole((experts, 2 * capacity, 2 * tok_count)),
                   whole((2,) + up_weight.shape[1:])],
        out_shape=[
            jax.ShapeDtypeStruct((experts, 2 * capacity, width), jnp.bfloat16),
            jax.ShapeDtypeStruct((experts, 2 * capacity, 2 * tok_count), jnp.bfloat16),
            jax.ShapeDtypeStruct((2,) + up_weight.shape[1:], up_weight.dtype),
        ],
    )(tokens, cotangent, modality.reshape(tok_count, 1), modal_gains, routes.T, gate_share.reshape(1, tok_count),
      up_weight, down_weight)


def on_device(tokens, modality, modal_gains, routes, gate_share, up_weight, down_weight, cotangent):
    tok_count = tokens.shape[0]
    model_width = tokens.shape[1]
    expert_count = lax.axis_size("expert")
    replica_count = lax.axis_size("dp")
    capacity = 4 * tok_count // expert_count
    slot_count = expert_count * capacity
    grad_scale = 1.0 / math.sqrt(2 * tok_count * replica_count)
    sending, return_side, shard = prologue(
        tokens, cotangent, modality, modal_gains, routes, gate_share, up_weight, down_weight, expert_count, capacity
    )
    whole = lax.all_gather(shard, "dp", axis=1, tiled=True)
    arrived = lax.all_to_all(sending, "expert", split_axis=0, concat_axis=0, tiled=True)
    leaving, parts = expert_block(arrived, whole, grad_scale)
    back = lax.all_to_all(leaving, "expert", split_axis=0, concat_axis=0, tiled=True)
    parts = parts.transpose(1, 0, 2)
    grad_pair = lax.psum_scatter(parts, "dp", scatter_dimension=0, tiled=True)
    up_grad = grad_pair[:, 0][None]
    down_grad = grad_pair[:, 1][None]
    combined = row_contract(return_side.reshape(2 * slot_count, 2 * tok_count), back.reshape(2 * slot_count, model_width))
    x_float = tokens.astype(jnp.float32)
    inv_rms = lax.rsqrt(jnp.mean(x_float * x_float, axis=-1, keepdims=True) + 1e-06)
    gain_rows = jnp.where(modality[:, None] == 1, modal_gains[1][None, :], modal_gains[0][None, :])
    moe_output = combined[:tok_count].astype(jnp.bfloat16)
    normed_grad = combined[tok_count:]
    scaled = gain_rows * normed_grad
    token_grad = (
        inv_rms * scaled - x_float * inv_rms**3 * jnp.mean(x_float * scaled, axis=-1, keepdims=True)
    ).astype(jnp.bfloat16)
    return (moe_output, token_grad, up_grad, down_grad)


def solution(mesh):
    placed = (
        P(("dp", "expert"), None),
        P(("dp", "expert")),
        P(),
        P(("dp", "expert"), None),
        P(("dp", "expert")),
        P("expert", "dp", None),
        P("expert", "dp", None),
        P(("dp", "expert"), None),
    )
    return jax.shard_map(
        on_device,
        mesh=mesh,
        in_specs=placed,
        out_specs=(
            P(("dp", "expert"), None),
            P(("dp", "expert"), None),
            P("expert", "dp", None),
            P("expert", "dp", None),
        ),
        check_vma=False,
    )
```

```python
import math

import jax
import jax.numpy as jnp
from jax import lax
from jax.experimental import pallas as pl
from jax.experimental.pallas import tpu as pltpu
from jax.sharding import PartitionSpec as P

root_half = 0.7071067811865476
density = 0.3989422804014327


def gelu_value(values):
    return values * 0.5 * (1.0 + lax.erf(values * root_half))


def gelu_slope(values):
    return (
        0.5 * (1.0 + lax.erf(values * root_half))
        + values * jnp.exp(-0.5 * values * values) * density
    )


def row_product(left_side, right_side, right_axis):
    numbers = (((1,), (right_axis,)), ((), ()))
    return lax.dot_general(left_side, right_side, numbers, preferred_element_type=jnp.float32)


def row_contract(left_side, right_side):
    numbers = (((0,), (0,)), ((), ()))
    return lax.dot_general(left_side, right_side, numbers, preferred_element_type=jnp.float32)


def expert_body(arrived_ref, up_ref, down_ref, leaving_ref, grads_ref, out_acc, back_acc, *, scale):
    step = pl.program_id(0)
    @pl.when(step == 0)
    def _():
        out_acc[...] = jnp.zeros_like(out_acc)
        back_acc[...] = jnp.zeros_like(back_acc)
    sources, both, width = arrived_ref.shape
    capacity = both // 2
    x = arrived_ref[:, :capacity, :].reshape(sources * capacity, width)
    g = arrived_ref[:, capacity:, :].reshape(sources * capacity, width)
    up = up_ref[0]
    down = down_ref[0]
    pre_act = row_product(x, up, 1)
    half_cdf = 0.5 * (1.0 + lax.erf(pre_act * root_half))
    activated = (pre_act * half_cdf).astype(jnp.bfloat16)
    out_acc[...] += row_product(activated, down, 0)
    hidden_grad = row_product(g, down, 1)
    slope = half_cdf + pre_act * jnp.exp(-0.5 * pre_act * pre_act) * density
    pre_grad = (hidden_grad * slope).astype(jnp.bfloat16)
    back_acc[...] += row_product(pre_grad, up, 0)
    grads_ref[0] = (row_contract(pre_grad, x) * scale).astype(jnp.bfloat16)
    grads_ref[1] = (row_contract(activated, g) * scale).astype(jnp.bfloat16)
    @pl.when(step == pl.num_programs(0) - 1)
    def _():
        leaving_ref[:, :capacity, :] = out_acc[...].astype(jnp.bfloat16).reshape(sources, capacity, width)
        leaving_ref[:, capacity:, :] = back_acc[...].astype(jnp.bfloat16).reshape(sources, capacity, width)

def expert_block(arrived, whole, scale, tile=512):
    sources, both, width = arrived.shape
    capacity = both // 2
    rows = sources * capacity
    hidden = whole.shape[1]
    return pl.pallas_call(
        lambda *refs: expert_body(*refs, scale=scale),
        grid=(hidden // tile,),
        in_specs=[
            pl.BlockSpec((sources, both, width), lambda j: (0, 0, 0)),
            pl.BlockSpec((1, tile, width), lambda j: (0, j, 0)),
            pl.BlockSpec((1, tile, width), lambda j: (1, j, 0)),
        ],
        out_specs=[
            pl.BlockSpec((sources, both, width), lambda j: (0, 0, 0)),
            pl.BlockSpec((2, tile, width), lambda j: (0, j, 0)),
        ],
        out_shape=[
            jax.ShapeDtypeStruct((sources, both, width), jnp.bfloat16),
            jax.ShapeDtypeStruct((2, hidden, width), jnp.bfloat16),
        ],
        scratch_shapes=[pltpu.VMEM((rows, width), jnp.float32), pltpu.VMEM((rows, width), jnp.float32)],
        cost_estimate=pl.CostEstimate(flops=12 * rows * hidden * width, transcendentals=2 * rows * hidden,
                                      bytes_accessed=2 * (4 * rows * width + 4 * hidden * width)),
    )(arrived, whole, whole)


def prologue_body(tokens_ref, cot_ref, modality_ref, gains_ref, routes_ref, share_ref, send_ref, back_side_ref,
                  *, experts, capacity):
    tok_count, width = tokens_ref.shape
    slots = experts * capacity
    x = tokens_ref[...].astype(jnp.float32)
    inv_rms = lax.rsqrt(jnp.mean(x * x, axis=-1, keepdims=True) + 1e-06)
    gains = gains_ref[...]
    gain_rows = jnp.where(modality_ref[...] == 1, gains[1:2, :], gains[0:1, :])
    normed = (x * inv_rms * gain_rows).astype(jnp.bfloat16)
    routes = routes_ref[...]
    first = routes[0:1, :]
    second = routes[1:2, :]
    expert_ids = lax.broadcasted_iota(jnp.int32, (experts, tok_count), 0)
    hot_first = (first == expert_ids).astype(jnp.float32)
    hot_second = (second == expert_ids).astype(jnp.float32)
    rows = lax.broadcasted_iota(jnp.int32, (tok_count, tok_count), 0)
    cols = lax.broadcasted_iota(jnp.int32, (tok_count, tok_count), 1)
    after = (rows < cols).astype(jnp.bfloat16)
    earlier = jnp.dot((hot_first + hot_second).astype(jnp.bfloat16), after, preferred_element_type=jnp.float32)
    rank_first = jnp.sum(earlier * hot_first, axis=0, keepdims=True).astype(jnp.int32)
    rank_second = jnp.sum(earlier * hot_second, axis=0, keepdims=True).astype(jnp.int32)
    slot_ids = lax.broadcasted_iota(jnp.int32, (slots, tok_count), 0)
    hit_first = slot_ids == first * capacity + rank_first
    hit_second = slot_ids == second * capacity + rank_second
    gate_first = share_ref[...].astype(jnp.float32) / 16.0
    pick = (hit_first | hit_second).astype(jnp.bfloat16)
    weigh = jnp.where(hit_first, gate_first, jnp.where(hit_second, 1.0 - gate_first, 0.0)).astype(jnp.bfloat16)
    token_rows = jnp.dot(pick, normed, preferred_element_type=jnp.float32).astype(jnp.bfloat16)
    grad_rows = jnp.dot(weigh, cot_ref[...], preferred_element_type=jnp.float32).astype(jnp.bfloat16)
    send_ref[:, :capacity, :] = token_rows.reshape(experts, capacity, width)
    send_ref[:, capacity:, :] = grad_rows.reshape(experts, capacity, width)
    blank = jnp.zeros_like(pick)
    back_side_ref[:, :capacity, :] = jnp.concatenate([weigh, blank], axis=1).reshape(experts, capacity, 2 * tok_count)
    back_side_ref[:, capacity:, :] = jnp.concatenate([blank, pick], axis=1).reshape(experts, capacity, 2 * tok_count)


def prologue(tokens, cotangent, modality, modal_gains, routes, gate_share, experts, capacity):
    tok_count, width = tokens.shape
    whole = lambda shape: pl.BlockSpec(shape, lambda: (0,) * len(shape))
    return pl.pallas_call(
        lambda *refs: prologue_body(*refs, experts=experts, capacity=capacity),
        in_specs=[whole((tok_count, width)), whole((tok_count, width)), whole((tok_count, 1)), whole((2, width)),
                  whole((2, tok_count)), whole((1, tok_count))],
        out_specs=[whole((experts, 2 * capacity, width)), whole((experts, 2 * capacity, 2 * tok_count))],
        out_shape=[
            jax.ShapeDtypeStruct((experts, 2 * capacity, width), jnp.bfloat16),
            jax.ShapeDtypeStruct((experts, 2 * capacity, 2 * tok_count), jnp.bfloat16),
        ],
    )(tokens, cotangent, modality.reshape(tok_count, 1), modal_gains, routes.T, gate_share.reshape(1, tok_count))


def epilogue_body(back_ref, side_ref, tokens_ref, modality_ref, gains_ref, grads_ref, moe_ref, token_grad_ref,
                  up_ref, down_ref):
    up_ref[0] = grads_ref[0]
    down_ref[0] = grads_ref[1]
    tok_count, width = tokens_ref.shape
    sources, both, _ = back_ref.shape
    back = back_ref[...].reshape(sources * both, width)
    side = side_ref[...].reshape(sources * both, 2 * tok_count)
    combined = row_contract(side, back)
    moe_ref[...] = combined[:tok_count].astype(jnp.bfloat16)
    normed_grad = combined[tok_count:]
    x = tokens_ref[...].astype(jnp.float32)
    inv_rms = lax.rsqrt(jnp.mean(x * x, axis=-1, keepdims=True) + 1e-06)
    gains = gains_ref[...]
    gain_rows = jnp.where(modality_ref[...] == 1, gains[1:2, :], gains[0:1, :])
    scaled = gain_rows * normed_grad
    token_grad_ref[...] = (
        inv_rms * scaled - x * inv_rms**3 * jnp.mean(x * scaled, axis=-1, keepdims=True)
    ).astype(jnp.bfloat16)


def epilogue(back, side, tokens, modality, modal_gains, grads):
    tok_count, width = tokens.shape
    whole = lambda shape: pl.BlockSpec(shape, lambda: (0,) * len(shape))
    one = (1,) + grads.shape[1:]
    return pl.pallas_call(
        epilogue_body,
        in_specs=[whole(back.shape), whole(side.shape), whole(tokens.shape), whole((tok_count, 1)),
                  whole(modal_gains.shape), whole(grads.shape)],
        out_specs=[whole(tokens.shape), whole(tokens.shape), whole(one), whole(one)],
        out_shape=[
            jax.ShapeDtypeStruct(tokens.shape, jnp.bfloat16),
            jax.ShapeDtypeStruct(tokens.shape, jnp.bfloat16),
            jax.ShapeDtypeStruct(one, grads.dtype),
            jax.ShapeDtypeStruct(one, grads.dtype),
        ],
    )(back, side, tokens, modality.reshape(tok_count, 1), modal_gains, grads)


def on_device(tokens, modality, modal_gains, routes, gate_share, up_weight, down_weight, cotangent):
    tok_count = tokens.shape[0]
    model_width = tokens.shape[1]
    expert_count = lax.axis_size("expert")
    replica_count = lax.axis_size("dp")
    capacity = 4 * tok_count // expert_count
    slot_count = expert_count * capacity
    route_count = 2 * tok_count
    grad_scale = 1.0 / math.sqrt(2 * tok_count * replica_count)
    whole = lax.all_gather(jnp.concatenate([up_weight, down_weight], axis=0), "dp", axis=1, tiled=True)
    sending, return_side = prologue(tokens, cotangent, modality, modal_gains, routes, gate_share, expert_count, capacity)
    arrived = lax.all_to_all(sending, "expert", split_axis=0, concat_axis=0, tiled=True)
    leaving, parts = expert_block(arrived, whole, grad_scale)
    back = lax.all_to_all(leaving, "expert", split_axis=0, concat_axis=0, tiled=True)
    grad_pair = lax.psum_scatter(parts, "dp", scatter_dimension=1, tiled=True)
    moe_output, token_grad, up_grad, down_grad = epilogue(back, return_side, tokens, modality, modal_gains, grad_pair)
    return (moe_output, token_grad, up_grad, down_grad)


def solution(mesh):
    placed = (
        P(("dp", "expert"), None),
        P(("dp", "expert")),
        P(),
        P(("dp", "expert"), None),
        P(("dp", "expert")),
        P("expert", "dp", None),
        P("expert", "dp", None),
        P(("dp", "expert"), None),
    )
    return jax.shard_map(
        on_device,
        mesh=mesh,
        in_specs=placed,
        out_specs=(
            P(("dp", "expert"), None),
            P(("dp", "expert"), None),
            P("expert", "dp", None),
            P("expert", "dp", None),
        ),
        check_vma=False,
    )
```

```python
import math

import jax
import jax.numpy as jnp
from jax import lax
from jax.experimental import pallas as pl
from jax.experimental.pallas import tpu as pltpu
from jax.sharding import PartitionSpec as P

root_half = 0.7071067811865476
density = 0.3989422804014327


def gelu_value(values):
    return values * 0.5 * (1.0 + lax.erf(values * root_half))


def gelu_slope(values):
    return (
        0.5 * (1.0 + lax.erf(values * root_half))
        + values * jnp.exp(-0.5 * values * values) * density
    )


def row_product(left_side, right_side, right_axis):
    numbers = (((1,), (right_axis,)), ((), ()))
    return lax.dot_general(left_side, right_side, numbers, preferred_element_type=jnp.float32)


def row_contract(left_side, right_side):
    numbers = (((0,), (0,)), ((), ()))
    return lax.dot_general(left_side, right_side, numbers, preferred_element_type=jnp.float32)


def expert_body(arrived_ref, up_ref, down_ref, leaving_ref, grads_ref, out_acc, back_acc, *, scale):
    step = pl.program_id(0)
    @pl.when(step == 0)
    def _():
        out_acc[...] = jnp.zeros_like(out_acc)
        back_acc[...] = jnp.zeros_like(back_acc)
    sources, both, width = arrived_ref.shape
    capacity = both // 2
    x = arrived_ref[:, :capacity, :].reshape(sources * capacity, width)
    g = arrived_ref[:, capacity:, :].reshape(sources * capacity, width)
    up = up_ref[0]
    down = down_ref[0]
    pre_act = row_product(x, up, 1)
    half_cdf = 0.5 * (1.0 + lax.erf(pre_act * root_half))
    activated = (pre_act * half_cdf).astype(jnp.bfloat16)
    out_acc[...] += row_product(activated, down, 0)
    hidden_grad = row_product(g, down, 1)
    slope = half_cdf + pre_act * jnp.exp(-0.5 * pre_act * pre_act) * density
    pre_grad = (hidden_grad * slope).astype(jnp.bfloat16)
    back_acc[...] += row_product(pre_grad, up, 0)
    grads_ref[0] = (row_contract(pre_grad, x) * scale).astype(jnp.bfloat16)
    grads_ref[1] = (row_contract(activated, g) * scale).astype(jnp.bfloat16)
    @pl.when(step == pl.num_programs(0) - 1)
    def _():
        leaving_ref[:, :capacity, :] = out_acc[...].astype(jnp.bfloat16).reshape(sources, capacity, width)
        leaving_ref[:, capacity:, :] = back_acc[...].astype(jnp.bfloat16).reshape(sources, capacity, width)

def expert_block(arrived, whole, scale, tile=512):
    sources, both, width = arrived.shape
    capacity = both // 2
    rows = sources * capacity
    hidden = whole.shape[1]
    return pl.pallas_call(
        lambda *refs: expert_body(*refs, scale=scale),
        grid=(hidden // tile,),
        in_specs=[
            pl.BlockSpec((sources, both, width), lambda j: (0, 0, 0)),
            pl.BlockSpec((1, tile, width), lambda j: (0, j, 0)),
            pl.BlockSpec((1, tile, width), lambda j: (1, j, 0)),
        ],
        out_specs=[
            pl.BlockSpec((sources, both, width), lambda j: (0, 0, 0)),
            pl.BlockSpec((2, tile, width), lambda j: (0, j, 0)),
        ],
        out_shape=[
            jax.ShapeDtypeStruct((sources, both, width), jnp.bfloat16),
            jax.ShapeDtypeStruct((2, hidden, width), jnp.bfloat16),
        ],
        scratch_shapes=[pltpu.VMEM((rows, width), jnp.float32), pltpu.VMEM((rows, width), jnp.float32)],
        cost_estimate=pl.CostEstimate(flops=12 * rows * hidden * width, transcendentals=2 * rows * hidden,
                                      bytes_accessed=2 * (4 * rows * width + 4 * hidden * width)),
    )(arrived, whole, whole)


def prologue_body(tokens_ref, cot_ref, modality_ref, gains_ref, routes_ref, share_ref, send_ref, back_side_ref,
                  *, experts, capacity):
    tok_count, width = tokens_ref.shape
    slots = experts * capacity
    x = tokens_ref[...].astype(jnp.float32)
    inv_rms = lax.rsqrt(jnp.mean(x * x, axis=-1, keepdims=True) + 1e-06)
    gains = gains_ref[...]
    gain_rows = jnp.where(modality_ref[...] == 1, gains[1:2, :], gains[0:1, :])
    normed = (x * inv_rms * gain_rows).astype(jnp.bfloat16)
    routes = routes_ref[...]
    first = routes[0:1, :]
    second = routes[1:2, :]
    expert_ids = lax.broadcasted_iota(jnp.int32, (experts, tok_count), 0)
    hot_first = (first == expert_ids).astype(jnp.float32)
    hot_second = (second == expert_ids).astype(jnp.float32)
    rows = lax.broadcasted_iota(jnp.int32, (tok_count, tok_count), 0)
    cols = lax.broadcasted_iota(jnp.int32, (tok_count, tok_count), 1)
    after = (rows < cols).astype(jnp.bfloat16)
    earlier = jnp.dot((hot_first + hot_second).astype(jnp.bfloat16), after, preferred_element_type=jnp.float32)
    rank_first = jnp.sum(earlier * hot_first, axis=0, keepdims=True).astype(jnp.int32)
    rank_second = jnp.sum(earlier * hot_second, axis=0, keepdims=True).astype(jnp.int32)
    slot_ids = lax.broadcasted_iota(jnp.int32, (slots, tok_count), 0)
    hit_first = slot_ids == first * capacity + rank_first
    hit_second = slot_ids == second * capacity + rank_second
    gate_first = share_ref[...].astype(jnp.float32) / 16.0
    pick = (hit_first | hit_second).astype(jnp.bfloat16)
    weigh = jnp.where(hit_first, gate_first, jnp.where(hit_second, 1.0 - gate_first, 0.0)).astype(jnp.bfloat16)
    token_rows = jnp.dot(pick, normed, preferred_element_type=jnp.float32).astype(jnp.bfloat16)
    grad_rows = jnp.dot(weigh, cot_ref[...], preferred_element_type=jnp.float32).astype(jnp.bfloat16)
    send_ref[:, :capacity, :] = token_rows.reshape(experts, capacity, width)
    send_ref[:, capacity:, :] = grad_rows.reshape(experts, capacity, width)
    blank = jnp.zeros_like(pick)
    back_side_ref[:, :capacity, :] = jnp.concatenate([weigh, blank], axis=1).reshape(experts, capacity, 2 * tok_count)
    back_side_ref[:, capacity:, :] = jnp.concatenate([blank, pick], axis=1).reshape(experts, capacity, 2 * tok_count)


def prologue(tokens, cotangent, modality, modal_gains, routes, gate_share, experts, capacity):
    tok_count, width = tokens.shape
    whole = lambda shape: pl.BlockSpec(shape, lambda: (0,) * len(shape))
    return pl.pallas_call(
        lambda *refs: prologue_body(*refs, experts=experts, capacity=capacity),
        in_specs=[whole((tok_count, width)), whole((tok_count, width)), whole((tok_count, 1)), whole((2, width)),
                  whole((2, tok_count)), whole((1, tok_count))],
        out_specs=[whole((experts, 2 * capacity, width)), whole((experts, 2 * capacity, 2 * tok_count))],
        out_shape=[
            jax.ShapeDtypeStruct((experts, 2 * capacity, width), jnp.bfloat16),
            jax.ShapeDtypeStruct((experts, 2 * capacity, 2 * tok_count), jnp.bfloat16),
        ],
    )(tokens, cotangent, modality.reshape(tok_count, 1), modal_gains, routes.T, gate_share.reshape(1, tok_count))


def on_device(tokens, modality, modal_gains, routes, gate_share, up_weight, down_weight, cotangent):
    tok_count = tokens.shape[0]
    model_width = tokens.shape[1]
    expert_count = lax.axis_size("z") * lax.axis_size("y")
    rings = lax.axis_size("z")
    replica_count = lax.axis_size("dp")
    capacity = 4 * tok_count // expert_count
    slot_count = expert_count * capacity
    route_count = 2 * tok_count
    grad_scale = 1.0 / math.sqrt(2 * tok_count * replica_count)
    whole = lax.all_gather(jnp.concatenate([up_weight, down_weight], axis=0), "dp", axis=1, tiled=True)
    sending, return_side = prologue(tokens, cotangent, modality, modal_gains, routes, gate_share, expert_count, capacity)
    staged = sending.reshape(rings, expert_count // rings, 2 * capacity, model_width)
    staged = lax.all_to_all(staged, "z", split_axis=0, concat_axis=0, tiled=True)
    staged = lax.all_to_all(staged, "y", split_axis=1, concat_axis=1, tiled=True)
    arrived = staged.reshape(expert_count, 2 * capacity, model_width)
    leaving, parts = expert_block(arrived, whole, grad_scale)
    staged = leaving.reshape(rings, expert_count // rings, 2 * capacity, model_width)
    staged = lax.all_to_all(staged, "y", split_axis=1, concat_axis=1, tiled=True)
    back = lax.all_to_all(staged, "z", split_axis=0, concat_axis=0, tiled=True)
    parts = parts.transpose(1, 0, 2)
    grad_pair = lax.psum_scatter(parts, "dp", scatter_dimension=0, tiled=True)
    up_grad = grad_pair[:, 0][None]
    down_grad = grad_pair[:, 1][None]
    combined = row_contract(return_side.reshape(2 * slot_count, 2 * tok_count), back.reshape(2 * slot_count, model_width))
    x_float = tokens.astype(jnp.float32)
    inv_rms = lax.rsqrt(jnp.mean(x_float * x_float, axis=-1, keepdims=True) + 1e-06)
    gain_rows = jnp.where(modality[:, None] == 1, modal_gains[1][None, :], modal_gains[0][None, :])
    moe_output = combined[:tok_count].astype(jnp.bfloat16)
    normed_grad = combined[tok_count:]
    scaled = gain_rows * normed_grad
    token_grad = (
        inv_rms * scaled - x_float * inv_rms**3 * jnp.mean(x_float * scaled, axis=-1, keepdims=True)
    ).astype(jnp.bfloat16)
    return (moe_output, token_grad, up_grad, down_grad)


def solution(mesh):
    dp_size, expert_size = mesh.devices.shape
    rings = math.isqrt(expert_size)
    mesh = jax.sharding.Mesh(mesh.devices.reshape(dp_size, rings, expert_size // rings), ("dp", "z", "y"))
    placed = (
        P(("dp", "z", "y"), None),
        P(("dp", "z", "y")),
        P(),
        P(("dp", "z", "y"), None),
        P(("dp", "z", "y")),
        P(("z", "y"), "dp", None),
        P(("z", "y"), "dp", None),
        P(("dp", "z", "y"), None),
    )
    return jax.shard_map(
        on_device,
        mesh=mesh,
        in_specs=placed,
        out_specs=(
            P(("dp", "z", "y"), None),
            P(("dp", "z", "y"), None),
            P(("z", "y"), "dp", None),
            P(("z", "y"), "dp", None),
        ),
        check_vma=False,
    )
```

```python
import math

import jax
import jax.numpy as jnp
from jax import lax
from jax.experimental import pallas as pl
from jax.experimental.pallas import tpu as pltpu
from jax.sharding import PartitionSpec as P

root_half = 0.7071067811865476
density = 0.3989422804014327


def gelu_value(values):
    return values * 0.5 * (1.0 + lax.erf(values * root_half))


def gelu_slope(values):
    return (
        0.5 * (1.0 + lax.erf(values * root_half))
        + values * jnp.exp(-0.5 * values * values) * density
    )


def row_product(left_side, right_side, right_axis):
    numbers = (((1,), (right_axis,)), ((), ()))
    return lax.dot_general(left_side, right_side, numbers, preferred_element_type=jnp.float32)


def row_contract(left_side, right_side):
    numbers = (((0,), (0,)), ((), ()))
    return lax.dot_general(left_side, right_side, numbers, preferred_element_type=jnp.float32)


def expert_body(arrived_ref, up_ref, down_ref, leaving_ref, grads_ref, out_acc, back_acc, *, scale):
    step = pl.program_id(0)
    @pl.when(step == 0)
    def _():
        out_acc[...] = jnp.zeros_like(out_acc)
        back_acc[...] = jnp.zeros_like(back_acc)
    sources, both, width = arrived_ref.shape
    capacity = both // 2
    x = arrived_ref[:, :capacity, :].reshape(sources * capacity, width)
    g = arrived_ref[:, capacity:, :].reshape(sources * capacity, width)
    up = up_ref[...]
    down = down_ref[...]
    pre_act = row_product(x, up, 1)
    half_cdf = 0.5 * (1.0 + lax.erf(pre_act * root_half))
    activated = (pre_act * half_cdf).astype(jnp.bfloat16)
    out_acc[...] += row_product(activated, down, 0)
    hidden_grad = row_product(g, down, 1)
    slope = half_cdf + pre_act * jnp.exp(-0.5 * pre_act * pre_act) * density
    pre_grad = (hidden_grad * slope).astype(jnp.bfloat16)
    back_acc[...] += row_product(pre_grad, up, 0)
    grads_ref[:, :width] = (row_contract(pre_grad, x) * scale).astype(jnp.bfloat16)
    grads_ref[:, width:] = (row_contract(activated, g) * scale).astype(jnp.bfloat16)
    @pl.when(step == pl.num_programs(0) - 1)
    def _():
        leaving_ref[:, :capacity, :] = out_acc[...].astype(jnp.bfloat16).reshape(sources, capacity, width)
        leaving_ref[:, capacity:, :] = back_acc[...].astype(jnp.bfloat16).reshape(sources, capacity, width)

def expert_block(arrived, whole, scale, tile=512):
    sources, both, width = arrived.shape
    capacity = both // 2
    rows = sources * capacity
    hidden = whole.shape[0]
    return pl.pallas_call(
        lambda *refs: expert_body(*refs, scale=scale),
        grid=(hidden // tile,),
        in_specs=[
            pl.BlockSpec((sources, both, width), lambda j: (0, 0, 0)),
            pl.BlockSpec((tile, width), lambda j: (j, 0)),
            pl.BlockSpec((tile, width), lambda j: (j, 1)),
        ],
        out_specs=[
            pl.BlockSpec((sources, both, width), lambda j: (0, 0, 0)),
            pl.BlockSpec((tile, 2 * width), lambda j: (j, 0)),
        ],
        out_shape=[
            jax.ShapeDtypeStruct((sources, both, width), jnp.bfloat16),
            jax.ShapeDtypeStruct((hidden, 2 * width), jnp.bfloat16),
        ],
        scratch_shapes=[pltpu.VMEM((rows, width), jnp.float32), pltpu.VMEM((rows, width), jnp.float32)],
        cost_estimate=pl.CostEstimate(flops=12 * rows * hidden * width, transcendentals=2 * rows * hidden,
                                      bytes_accessed=2 * (4 * rows * width + 4 * hidden * width)),
    )(arrived, whole, whole)


def prologue_body(tokens_ref, cot_ref, modality_ref, gains_ref, routes_ref, share_ref, send_ref, back_side_ref,
                  *, experts, capacity):
    tok_count, width = tokens_ref.shape
    slots = experts * capacity
    x = tokens_ref[...].astype(jnp.float32)
    inv_rms = lax.rsqrt(jnp.mean(x * x, axis=-1, keepdims=True) + 1e-06)
    gains = gains_ref[...]
    gain_rows = jnp.where(modality_ref[...] == 1, gains[1:2, :], gains[0:1, :])
    normed = (x * inv_rms * gain_rows).astype(jnp.bfloat16)
    routes = routes_ref[...]
    first = routes[0:1, :]
    second = routes[1:2, :]
    expert_ids = lax.broadcasted_iota(jnp.int32, (experts, tok_count), 0)
    hot_first = (first == expert_ids).astype(jnp.float32)
    hot_second = (second == expert_ids).astype(jnp.float32)
    rows = lax.broadcasted_iota(jnp.int32, (tok_count, tok_count), 0)
    cols = lax.broadcasted_iota(jnp.int32, (tok_count, tok_count), 1)
    after = (rows < cols).astype(jnp.bfloat16)
    earlier = jnp.dot((hot_first + hot_second).astype(jnp.bfloat16), after, preferred_element_type=jnp.float32)
    rank_first = jnp.sum(earlier * hot_first, axis=0, keepdims=True).astype(jnp.int32)
    rank_second = jnp.sum(earlier * hot_second, axis=0, keepdims=True).astype(jnp.int32)
    slot_ids = lax.broadcasted_iota(jnp.int32, (slots, tok_count), 0)
    hit_first = slot_ids == first * capacity + rank_first
    hit_second = slot_ids == second * capacity + rank_second
    gate_first = share_ref[...].astype(jnp.float32) / 16.0
    pick = (hit_first | hit_second).astype(jnp.bfloat16)
    weigh = jnp.where(hit_first, gate_first, jnp.where(hit_second, 1.0 - gate_first, 0.0)).astype(jnp.bfloat16)
    token_rows = jnp.dot(pick, normed, preferred_element_type=jnp.float32).astype(jnp.bfloat16)
    grad_rows = jnp.dot(weigh, cot_ref[...], preferred_element_type=jnp.float32).astype(jnp.bfloat16)
    send_ref[:, :capacity, :] = token_rows.reshape(experts, capacity, width)
    send_ref[:, capacity:, :] = grad_rows.reshape(experts, capacity, width)
    blank = jnp.zeros_like(pick)
    back_side_ref[:, :capacity, :] = jnp.concatenate([weigh, blank], axis=1).reshape(experts, capacity, 2 * tok_count)
    back_side_ref[:, capacity:, :] = jnp.concatenate([blank, pick], axis=1).reshape(experts, capacity, 2 * tok_count)


def prologue(tokens, cotangent, modality, modal_gains, routes, gate_share, experts, capacity):
    tok_count, width = tokens.shape
    whole = lambda shape: pl.BlockSpec(shape, lambda: (0,) * len(shape))
    return pl.pallas_call(
        lambda *refs: prologue_body(*refs, experts=experts, capacity=capacity),
        in_specs=[whole((tok_count, width)), whole((tok_count, width)), whole((tok_count, 1)), whole((2, width)),
                  whole((2, tok_count)), whole((1, tok_count))],
        out_specs=[whole((experts, 2 * capacity, width)), whole((experts, 2 * capacity, 2 * tok_count))],
        out_shape=[
            jax.ShapeDtypeStruct((experts, 2 * capacity, width), jnp.bfloat16),
            jax.ShapeDtypeStruct((experts, 2 * capacity, 2 * tok_count), jnp.bfloat16),
        ],
    )(tokens, cotangent, modality.reshape(tok_count, 1), modal_gains, routes.T, gate_share.reshape(1, tok_count))


def on_device(tokens, modality, modal_gains, routes, gate_share, up_weight, down_weight, cotangent):
    tok_count = tokens.shape[0]
    model_width = tokens.shape[1]
    expert_count = lax.axis_size("expert")
    replica_count = lax.axis_size("dp")
    capacity = 4 * tok_count // expert_count
    slot_count = expert_count * capacity
    route_count = 2 * tok_count
    grad_scale = 1.0 / math.sqrt(2 * tok_count * replica_count)
    whole = lax.all_gather(jnp.concatenate([up_weight[0], down_weight[0]], axis=1), "dp", axis=0, tiled=True)
    sending, return_side = prologue(tokens, cotangent, modality, modal_gains, routes, gate_share, expert_count, capacity)
    arrived = lax.all_to_all(sending, "expert", split_axis=0, concat_axis=0, tiled=True)
    leaving, parts = expert_block(arrived, whole, grad_scale)
    back = lax.all_to_all(leaving, "expert", split_axis=0, concat_axis=0, tiled=True)
    grad_pair = lax.psum_scatter(parts, "dp", scatter_dimension=0, tiled=True)
    up_grad = grad_pair[:, :model_width][None]
    down_grad = grad_pair[:, model_width:][None]
    combined = row_contract(return_side.reshape(2 * slot_count, 2 * tok_count), back.reshape(2 * slot_count, model_width))
    x_float = tokens.astype(jnp.float32)
    inv_rms = lax.rsqrt(jnp.mean(x_float * x_float, axis=-1, keepdims=True) + 1e-06)
    gain_rows = jnp.where(modality[:, None] == 1, modal_gains[1][None, :], modal_gains[0][None, :])
    moe_output = combined[:tok_count].astype(jnp.bfloat16)
    normed_grad = combined[tok_count:]
    scaled = gain_rows * normed_grad
    token_grad = (
        inv_rms * scaled - x_float * inv_rms**3 * jnp.mean(x_float * scaled, axis=-1, keepdims=True)
    ).astype(jnp.bfloat16)
    return (moe_output, token_grad, up_grad, down_grad)


def solution(mesh):
    placed = (
        P(("dp", "expert"), None),
        P(("dp", "expert")),
        P(),
        P(("dp", "expert"), None),
        P(("dp", "expert")),
        P("expert", "dp", None),
        P("expert", "dp", None),
        P(("dp", "expert"), None),
    )
    return jax.shard_map(
        on_device,
        mesh=mesh,
        in_specs=placed,
        out_specs=(
            P(("dp", "expert"), None),
            P(("dp", "expert"), None),
            P("expert", "dp", None),
            P("expert", "dp", None),
        ),
        check_vma=False,
    )
```

```python
import math

import jax
import jax.numpy as jnp
from jax import lax
from jax.experimental import pallas as pl
from jax.experimental.pallas import tpu as pltpu
from jax.sharding import PartitionSpec as P

root_half = 0.7071067811865476
density = 0.3989422804014327


def gelu_value(values):
    return values * 0.5 * (1.0 + lax.erf(values * root_half))


def gelu_slope(values):
    return (
        0.5 * (1.0 + lax.erf(values * root_half))
        + values * jnp.exp(-0.5 * values * values) * density
    )


def row_product(left_side, right_side, right_axis):
    numbers = (((1,), (right_axis,)), ((), ()))
    return lax.dot_general(left_side, right_side, numbers, preferred_element_type=jnp.float32)


def row_contract(left_side, right_side):
    numbers = (((0,), (0,)), ((), ()))
    return lax.dot_general(left_side, right_side, numbers, preferred_element_type=jnp.float32)


def expert_body(arrived_ref, up_ref, down_ref, leaving_ref, grads_ref, out_acc, back_acc, *, scale):
    step = pl.program_id(0)
    @pl.when(step == 0)
    def _():
        out_acc[...] = jnp.zeros_like(out_acc)
        back_acc[...] = jnp.zeros_like(back_acc)
    sources, both, width = arrived_ref.shape
    capacity = both // 2
    x = arrived_ref[:, :capacity, :].reshape(sources * capacity, width)
    g = arrived_ref[:, capacity:, :].reshape(sources * capacity, width)
    up = up_ref[0]
    down = down_ref[0]
    pre_act = row_product(x, up, 1)
    half_cdf = 0.5 * (1.0 + lax.erf(pre_act * root_half))
    activated = (pre_act * half_cdf).astype(jnp.bfloat16)
    out_acc[...] += row_product(activated, down, 0)
    hidden_grad = row_product(g, down, 1)
    slope = half_cdf + pre_act * jnp.exp(-0.5 * pre_act * pre_act) * density
    pre_grad = (hidden_grad * slope).astype(jnp.bfloat16)
    back_acc[...] += row_product(pre_grad, up, 0)
    grads_ref[0] = (row_contract(pre_grad, x) * scale).astype(jnp.bfloat16)
    grads_ref[1] = (row_contract(activated, g) * scale).astype(jnp.bfloat16)
    @pl.when(step == pl.num_programs(0) - 1)
    def _():
        leaving_ref[:, :capacity, :] = out_acc[...].astype(jnp.bfloat16).reshape(sources, capacity, width)
        leaving_ref[:, capacity:, :] = back_acc[...].astype(jnp.bfloat16).reshape(sources, capacity, width)

def expert_block(arrived, whole, scale, tile=512):
    sources, both, width = arrived.shape
    capacity = both // 2
    rows = sources * capacity
    hidden = whole.shape[1]
    return pl.pallas_call(
        lambda *refs: expert_body(*refs, scale=scale),
        grid=(hidden // tile,),
        in_specs=[
            pl.BlockSpec((sources, both, width), lambda j: (0, 0, 0)),
            pl.BlockSpec((1, tile, width), lambda j: (0, j, 0)),
            pl.BlockSpec((1, tile, width), lambda j: (1, j, 0)),
        ],
        out_specs=[
            pl.BlockSpec((sources, both, width), lambda j: (0, 0, 0)),
            pl.BlockSpec((2, tile, width), lambda j: (0, j, 0)),
        ],
        out_shape=[
            jax.ShapeDtypeStruct((sources, both, width), jnp.bfloat16),
            jax.ShapeDtypeStruct((2, hidden, width), jnp.bfloat16),
        ],
        scratch_shapes=[pltpu.VMEM((rows, width), jnp.float32), pltpu.VMEM((rows, width), jnp.float32)],
        cost_estimate=pl.CostEstimate(flops=12 * rows * hidden * width, transcendentals=2 * rows * hidden,
                                      bytes_accessed=2 * (4 * rows * width + 4 * hidden * width)),
    )(arrived, whole, whole)


def prologue_body(tokens_ref, cot_ref, modality_ref, gains_ref, routes_ref, share_ref, send_ref, back_side_ref,
                  *, experts, capacity):
    tok_count, width = tokens_ref.shape
    slots = experts * capacity
    x = tokens_ref[...].astype(jnp.float32)
    inv_rms = lax.rsqrt(jnp.mean(x * x, axis=-1, keepdims=True) + 1e-06)
    gains = gains_ref[...]
    gain_rows = jnp.where(modality_ref[...] == 1, gains[1:2, :], gains[0:1, :])
    normed = (x * inv_rms * gain_rows).astype(jnp.bfloat16)
    routes = routes_ref[...]
    first = routes[0:1, :]
    second = routes[1:2, :]
    expert_ids = lax.broadcasted_iota(jnp.int32, (experts, tok_count), 0)
    hot_first = (first == expert_ids).astype(jnp.float32)
    hot_second = (second == expert_ids).astype(jnp.float32)
    rows = lax.broadcasted_iota(jnp.int32, (tok_count, tok_count), 0)
    cols = lax.broadcasted_iota(jnp.int32, (tok_count, tok_count), 1)
    after = (rows < cols).astype(jnp.bfloat16)
    earlier = jnp.dot((hot_first + hot_second).astype(jnp.bfloat16), after, preferred_element_type=jnp.float32)
    rank_first = jnp.sum(earlier * hot_first, axis=0, keepdims=True).astype(jnp.int32)
    rank_second = jnp.sum(earlier * hot_second, axis=0, keepdims=True).astype(jnp.int32)
    slot_ids = lax.broadcasted_iota(jnp.int32, (slots, tok_count), 0)
    hit_first = slot_ids == first * capacity + rank_first
    hit_second = slot_ids == second * capacity + rank_second
    gate_first = share_ref[...].astype(jnp.float32) / 16.0
    pick = (hit_first | hit_second).astype(jnp.bfloat16)
    weigh = jnp.where(hit_first, gate_first, jnp.where(hit_second, 1.0 - gate_first, 0.0)).astype(jnp.bfloat16)
    token_rows = jnp.dot(pick, normed, preferred_element_type=jnp.float32).astype(jnp.bfloat16)
    grad_rows = jnp.dot(weigh, cot_ref[...], preferred_element_type=jnp.float32).astype(jnp.bfloat16)
    send_ref[:, :capacity, :] = token_rows.reshape(experts, capacity, width)
    send_ref[:, capacity:, :] = grad_rows.reshape(experts, capacity, width)
    blank = jnp.zeros_like(pick)
    back_side_ref[:, :capacity, :] = jnp.concatenate([weigh, blank], axis=1).reshape(experts, capacity, 2 * tok_count)
    back_side_ref[:, capacity:, :] = jnp.concatenate([blank, pick], axis=1).reshape(experts, capacity, 2 * tok_count)


def prologue(tokens, cotangent, modality, modal_gains, routes, gate_share, experts, capacity):
    tok_count, width = tokens.shape
    whole = lambda shape: pl.BlockSpec(shape, lambda: (0,) * len(shape))
    return pl.pallas_call(
        lambda *refs: prologue_body(*refs, experts=experts, capacity=capacity),
        in_specs=[whole((tok_count, width)), whole((tok_count, width)), whole((tok_count, 1)), whole((2, width)),
                  whole((2, tok_count)), whole((1, tok_count))],
        out_specs=[whole((experts, 2 * capacity, width)), whole((experts, 2 * capacity, 2 * tok_count))],
        out_shape=[
            jax.ShapeDtypeStruct((experts, 2 * capacity, width), jnp.bfloat16),
            jax.ShapeDtypeStruct((experts, 2 * capacity, 2 * tok_count), jnp.bfloat16),
        ],
    )(tokens, cotangent, modality.reshape(tok_count, 1), modal_gains, routes.T, gate_share.reshape(1, tok_count))


def on_device(tokens, modality, modal_gains, routes, gate_share, up_weight, down_weight, cotangent):
    tok_count = tokens.shape[0]
    model_width = tokens.shape[1]
    expert_count = lax.axis_size("expert")
    replica_count = lax.axis_size("dp")
    capacity = 4 * tok_count // expert_count
    slot_count = expert_count * capacity
    route_count = 2 * tok_count
    grad_scale = 1.0 / math.sqrt(2 * tok_count * replica_count)
    whole = lax.all_gather(jnp.concatenate([up_weight, down_weight], axis=0), "dp", axis=1, tiled=True)
    sending, return_side = prologue(tokens, cotangent, modality, modal_gains, routes, gate_share, expert_count, capacity)
    arrived = lax.all_to_all(sending, "expert", split_axis=0, concat_axis=0, tiled=True)
    leaving, parts = expert_block(arrived, whole, grad_scale)
    back = lax.all_to_all(leaving, "expert", split_axis=0, concat_axis=0, tiled=True)
    parts = parts.transpose(1, 0, 2)
    grad_pair = lax.psum_scatter(parts, "dp", scatter_dimension=0, tiled=True)
    up_grad = grad_pair[:, 0][None]
    down_grad = grad_pair[:, 1][None]
    side = return_side.reshape(2 * slot_count, 2 * tok_count)
    returned = back.reshape(2 * slot_count, model_width)
    x_float = tokens.astype(jnp.float32)
    inv_rms = lax.rsqrt(jnp.mean(x_float * x_float, axis=-1, keepdims=True) + 1e-06)
    gain_rows = jnp.where(modality[:, None] == 1, modal_gains[1][None, :], modal_gains[0][None, :])
    moe_output = row_contract(side[:, :tok_count], returned).astype(jnp.bfloat16)
    normed_grad = row_contract(side[:, tok_count:], returned)
    scaled = gain_rows * normed_grad
    token_grad = (
        inv_rms * scaled - x_float * inv_rms**3 * jnp.mean(x_float * scaled, axis=-1, keepdims=True)
    ).astype(jnp.bfloat16)
    return (moe_output, token_grad, up_grad, down_grad)


def solution(mesh):
    placed = (
        P(("dp", "expert"), None),
        P(("dp", "expert")),
        P(),
        P(("dp", "expert"), None),
        P(("dp", "expert")),
        P("expert", "dp", None),
        P("expert", "dp", None),
        P(("dp", "expert"), None),
    )
    return jax.shard_map(
        on_device,
        mesh=mesh,
        in_specs=placed,
        out_specs=(
            P(("dp", "expert"), None),
            P(("dp", "expert"), None),
            P("expert", "dp", None),
            P("expert", "dp", None),
        ),
        check_vma=False,
    )
```

```python
import math

import jax
import jax.numpy as jnp
from jax import lax
from jax.experimental import pallas as pl
from jax.experimental.pallas import tpu as pltpu
from jax.sharding import PartitionSpec as P

root_half = 0.7071067811865476
density = 0.3989422804014327


def gelu_value(values):
    return values * 0.5 * (1.0 + lax.erf(values * root_half))


def gelu_slope(values):
    return (
        0.5 * (1.0 + lax.erf(values * root_half))
        + values * jnp.exp(-0.5 * values * values) * density
    )


def row_product(left_side, right_side, right_axis):
    numbers = (((1,), (right_axis,)), ((), ()))
    return lax.dot_general(left_side, right_side, numbers, preferred_element_type=jnp.float32)


def row_contract(left_side, right_side):
    numbers = (((0,), (0,)), ((), ()))
    return lax.dot_general(left_side, right_side, numbers, preferred_element_type=jnp.float32)


def expert_body(arrived_ref, up_ref, down_ref, leaving_ref, grads_ref, out_acc, back_acc, *, scale):
    step = pl.program_id(0)
    @pl.when(step == 0)
    def _():
        out_acc[...] = jnp.zeros_like(out_acc)
        back_acc[...] = jnp.zeros_like(back_acc)
    sources, both, width = arrived_ref.shape
    capacity = both // 2
    x = arrived_ref[:, :capacity, :].reshape(sources * capacity, width)
    g = arrived_ref[:, capacity:, :].reshape(sources * capacity, width)
    up = up_ref[0]
    down = down_ref[0]
    pre_act = row_product(x, up, 1)
    half_cdf = 0.5 * (1.0 + lax.erf(pre_act * root_half))
    activated = (pre_act * half_cdf).astype(jnp.bfloat16)
    out_acc[...] += row_product(activated, down, 0)
    hidden_grad = row_product(g, down, 1)
    slope = half_cdf + pre_act * jnp.exp(-0.5 * pre_act * pre_act) * density
    pre_grad = (hidden_grad * slope).astype(jnp.bfloat16)
    back_acc[...] += row_product(pre_grad, up, 0)
    grads_ref[0] = (row_contract(pre_grad, x) * scale).astype(jnp.bfloat16)
    grads_ref[1] = (row_contract(activated, g) * scale).astype(jnp.bfloat16)
    @pl.when(step == pl.num_programs(0) - 1)
    def _():
        leaving_ref[:, :capacity, :] = out_acc[...].astype(jnp.bfloat16).reshape(sources, capacity, width)
        leaving_ref[:, capacity:, :] = back_acc[...].astype(jnp.bfloat16).reshape(sources, capacity, width)

def expert_block(arrived, whole, scale, tile=1024):
    sources, both, width = arrived.shape
    capacity = both // 2
    rows = sources * capacity
    hidden = whole.shape[1]
    return pl.pallas_call(
        lambda *refs: expert_body(*refs, scale=scale),
        grid=(hidden // tile,),
        in_specs=[
            pl.BlockSpec((sources, both, width), lambda j: (0, 0, 0)),
            pl.BlockSpec((1, tile, width), lambda j: (0, j, 0)),
            pl.BlockSpec((1, tile, width), lambda j: (1, j, 0)),
        ],
        out_specs=[
            pl.BlockSpec((sources, both, width), lambda j: (0, 0, 0)),
            pl.BlockSpec((2, tile, width), lambda j: (0, j, 0)),
        ],
        out_shape=[
            jax.ShapeDtypeStruct((sources, both, width), jnp.bfloat16),
            jax.ShapeDtypeStruct((2, hidden, width), jnp.bfloat16),
        ],
        scratch_shapes=[pltpu.VMEM((rows, width), jnp.float32), pltpu.VMEM((rows, width), jnp.float32)],
        cost_estimate=pl.CostEstimate(flops=12 * rows * hidden * width, transcendentals=2 * rows * hidden,
                                      bytes_accessed=2 * (4 * rows * width + 4 * hidden * width)),
    )(arrived, whole, whole)


def prologue_body(tokens_ref, cot_ref, modality_ref, gains_ref, routes_ref, share_ref, send_ref, back_side_ref,
                  *, experts, capacity):
    tok_count, width = tokens_ref.shape
    slots = experts * capacity
    x = tokens_ref[...].astype(jnp.float32)
    inv_rms = lax.rsqrt(jnp.mean(x * x, axis=-1, keepdims=True) + 1e-06)
    gains = gains_ref[...]
    gain_rows = jnp.where(modality_ref[...] == 1, gains[1:2, :], gains[0:1, :])
    normed = (x * inv_rms * gain_rows).astype(jnp.bfloat16)
    routes = routes_ref[...]
    first = routes[0:1, :]
    second = routes[1:2, :]
    expert_ids = lax.broadcasted_iota(jnp.int32, (experts, tok_count), 0)
    hot_first = (first == expert_ids).astype(jnp.float32)
    hot_second = (second == expert_ids).astype(jnp.float32)
    rows = lax.broadcasted_iota(jnp.int32, (tok_count, tok_count), 0)
    cols = lax.broadcasted_iota(jnp.int32, (tok_count, tok_count), 1)
    after = (rows < cols).astype(jnp.bfloat16)
    earlier = jnp.dot((hot_first + hot_second).astype(jnp.bfloat16), after, preferred_element_type=jnp.float32)
    rank_first = jnp.sum(earlier * hot_first, axis=0, keepdims=True).astype(jnp.int32)
    rank_second = jnp.sum(earlier * hot_second, axis=0, keepdims=True).astype(jnp.int32)
    slot_ids = lax.broadcasted_iota(jnp.int32, (slots, tok_count), 0)
    hit_first = slot_ids == first * capacity + rank_first
    hit_second = slot_ids == second * capacity + rank_second
    gate_first = share_ref[...].astype(jnp.float32) / 16.0
    pick = (hit_first | hit_second).astype(jnp.bfloat16)
    weigh = jnp.where(hit_first, gate_first, jnp.where(hit_second, 1.0 - gate_first, 0.0)).astype(jnp.bfloat16)
    token_rows = jnp.dot(pick, normed, preferred_element_type=jnp.float32).astype(jnp.bfloat16)
    grad_rows = jnp.dot(weigh, cot_ref[...], preferred_element_type=jnp.float32).astype(jnp.bfloat16)
    send_ref[:, :capacity, :] = token_rows.reshape(experts, capacity, width)
    send_ref[:, capacity:, :] = grad_rows.reshape(experts, capacity, width)
    blank = jnp.zeros_like(pick)
    back_side_ref[:, :capacity, :] = jnp.concatenate([weigh, blank], axis=1).reshape(experts, capacity, 2 * tok_count)
    back_side_ref[:, capacity:, :] = jnp.concatenate([blank, pick], axis=1).reshape(experts, capacity, 2 * tok_count)


def prologue(tokens, cotangent, modality, modal_gains, routes, gate_share, experts, capacity):
    tok_count, width = tokens.shape
    whole = lambda shape: pl.BlockSpec(shape, lambda: (0,) * len(shape))
    return pl.pallas_call(
        lambda *refs: prologue_body(*refs, experts=experts, capacity=capacity),
        in_specs=[whole((tok_count, width)), whole((tok_count, width)), whole((tok_count, 1)), whole((2, width)),
                  whole((2, tok_count)), whole((1, tok_count))],
        out_specs=[whole((experts, 2 * capacity, width)), whole((experts, 2 * capacity, 2 * tok_count))],
        out_shape=[
            jax.ShapeDtypeStruct((experts, 2 * capacity, width), jnp.bfloat16),
            jax.ShapeDtypeStruct((experts, 2 * capacity, 2 * tok_count), jnp.bfloat16),
        ],
    )(tokens, cotangent, modality.reshape(tok_count, 1), modal_gains, routes.T, gate_share.reshape(1, tok_count))


def on_device(tokens, modality, modal_gains, routes, gate_share, up_weight, down_weight, cotangent):
    tok_count = tokens.shape[0]
    model_width = tokens.shape[1]
    expert_count = lax.axis_size("expert")
    replica_count = lax.axis_size("dp")
    capacity = 4 * tok_count // expert_count
    slot_count = expert_count * capacity
    route_count = 2 * tok_count
    grad_scale = 1.0 / math.sqrt(2 * tok_count * replica_count)
    whole = lax.all_gather(jnp.concatenate([up_weight, down_weight], axis=0), "dp", axis=1, tiled=True)
    sending, return_side = prologue(tokens, cotangent, modality, modal_gains, routes, gate_share, expert_count, capacity)
    arrived = lax.all_to_all(sending, "expert", split_axis=0, concat_axis=0, tiled=True)
    leaving, parts = expert_block(arrived, whole, grad_scale)
    back = lax.all_to_all(leaving, "expert", split_axis=0, concat_axis=0, tiled=True)
    parts = parts.transpose(1, 0, 2)
    grad_pair = lax.psum_scatter(parts, "dp", scatter_dimension=0, tiled=True)
    up_grad = grad_pair[:, 0][None]
    down_grad = grad_pair[:, 1][None]
    side = return_side.reshape(2 * slot_count, 2 * tok_count)
    returned = back.reshape(2 * slot_count, model_width)
    x_float = tokens.astype(jnp.float32)
    inv_rms = lax.rsqrt(jnp.mean(x_float * x_float, axis=-1, keepdims=True) + 1e-06)
    gain_rows = jnp.where(modality[:, None] == 1, modal_gains[1][None, :], modal_gains[0][None, :])
    moe_output = row_contract(side[:, :tok_count], returned).astype(jnp.bfloat16)
    normed_grad = row_contract(side[:, tok_count:], returned)
    scaled = gain_rows * normed_grad
    token_grad = (
        inv_rms * scaled - x_float * inv_rms**3 * jnp.mean(x_float * scaled, axis=-1, keepdims=True)
    ).astype(jnp.bfloat16)
    return (moe_output, token_grad, up_grad, down_grad)


def solution(mesh):
    placed = (
        P(("dp", "expert"), None),
        P(("dp", "expert")),
        P(),
        P(("dp", "expert"), None),
        P(("dp", "expert")),
        P("expert", "dp", None),
        P("expert", "dp", None),
        P(("dp", "expert"), None),
    )
    return jax.shard_map(
        on_device,
        mesh=mesh,
        in_specs=placed,
        out_specs=(
            P(("dp", "expert"), None),
            P(("dp", "expert"), None),
            P("expert", "dp", None),
            P("expert", "dp", None),
        ),
        check_vma=False,
    )
```

```python
import math

import jax
import jax.numpy as jnp
from jax import lax
from jax.experimental import pallas as pl
from jax.experimental.pallas import tpu as pltpu
from jax.sharding import PartitionSpec as P

root_half = 0.7071067811865476
density = 0.3989422804014327


def gelu_value(values):
    return values * 0.5 * (1.0 + lax.erf(values * root_half))


def gelu_slope(values):
    return (
        0.5 * (1.0 + lax.erf(values * root_half))
        + values * jnp.exp(-0.5 * values * values) * density
    )


def row_product(left_side, right_side, right_axis):
    numbers = (((1,), (right_axis,)), ((), ()))
    return lax.dot_general(left_side, right_side, numbers, preferred_element_type=jnp.float32)


def row_contract(left_side, right_side):
    numbers = (((0,), (0,)), ((), ()))
    return lax.dot_general(left_side, right_side, numbers, preferred_element_type=jnp.float32)


def expert_body(arrived_ref, up_ref, down_ref, leaving_ref, grads_ref, out_acc, back_acc, *, scale):
    step = pl.program_id(0)
    @pl.when(step == 0)
    def _():
        out_acc[...] = jnp.zeros_like(out_acc)
        back_acc[...] = jnp.zeros_like(back_acc)
    sources, both, width = arrived_ref.shape
    capacity = both // 2
    x = arrived_ref[:, :capacity, :].reshape(sources * capacity, width)
    g = arrived_ref[:, capacity:, :].reshape(sources * capacity, width)
    up = up_ref[0]
    down = down_ref[0]
    pre_act = row_product(x, up, 1)
    half_cdf = 0.5 * (1.0 + lax.erf(pre_act * root_half))
    activated = (pre_act * half_cdf).astype(jnp.bfloat16)
    out_acc[...] += row_product(activated, down, 0)
    hidden_grad = row_product(g, down, 1)
    slope = half_cdf + pre_act * jnp.exp(-0.5 * pre_act * pre_act) * density
    pre_grad = (hidden_grad * slope).astype(jnp.bfloat16)
    back_acc[...] += row_product(pre_grad, up, 0)
    grads_ref[0] = (row_contract(pre_grad, x) * scale).astype(jnp.bfloat16)
    grads_ref[1] = (row_contract(activated, g) * scale).astype(jnp.bfloat16)
    @pl.when(step == pl.num_programs(0) - 1)
    def _():
        leaving_ref[:, :capacity, :] = out_acc[...].astype(jnp.bfloat16).reshape(sources, capacity, width)
        leaving_ref[:, capacity:, :] = back_acc[...].astype(jnp.bfloat16).reshape(sources, capacity, width)

def expert_block(arrived, whole, scale, tile=512):
    sources, both, width = arrived.shape
    capacity = both // 2
    rows = sources * capacity
    hidden = whole.shape[1]
    return pl.pallas_call(
        lambda *refs: expert_body(*refs, scale=scale),
        grid=(hidden // tile,),
        in_specs=[
            pl.BlockSpec((sources, both, width), lambda j: (0, 0, 0)),
            pl.BlockSpec((1, tile, width), lambda j: (0, j, 0)),
            pl.BlockSpec((1, tile, width), lambda j: (1, j, 0)),
        ],
        out_specs=[
            pl.BlockSpec((sources, both, width), lambda j: (0, 0, 0)),
            pl.BlockSpec((2, tile, width), lambda j: (0, j, 0)),
        ],
        out_shape=[
            jax.ShapeDtypeStruct((sources, both, width), jnp.bfloat16),
            jax.ShapeDtypeStruct((2, hidden, width), jnp.bfloat16),
        ],
        scratch_shapes=[pltpu.VMEM((rows, width), jnp.float32), pltpu.VMEM((rows, width), jnp.float32)],
        cost_estimate=pl.CostEstimate(flops=12 * rows * hidden * width, transcendentals=2 * rows * hidden,
                                      bytes_accessed=2 * (4 * rows * width + 4 * hidden * width)),
    )(arrived, whole, whole)


def prologue_body(tokens_ref, cot_ref, modality_ref, gains_ref, routes_ref, share_ref, send_ref, back_side_ref,
                  *, experts, capacity):
    tok_count, width = tokens_ref.shape
    slots = experts * capacity
    x = tokens_ref[...].astype(jnp.float32)
    inv_rms = lax.rsqrt(jnp.mean(x * x, axis=-1, keepdims=True) + 1e-06)
    gains = gains_ref[...]
    modality = jnp.transpose(jnp.broadcast_to(modality_ref[...].astype(jnp.float32), (tok_count, tok_count)))[:, 0:1]
    gain_rows = jnp.where(modality > 0.5, gains[1:2, :], gains[0:1, :])
    normed = (x * inv_rms * gain_rows).astype(jnp.bfloat16)
    routes = routes_ref[...]
    first = routes[0:1, :]
    second = routes[1:2, :]
    expert_ids = lax.broadcasted_iota(jnp.int32, (experts, tok_count), 0)
    hot_first = (first == expert_ids).astype(jnp.float32)
    hot_second = (second == expert_ids).astype(jnp.float32)
    rows = lax.broadcasted_iota(jnp.int32, (tok_count, tok_count), 0)
    cols = lax.broadcasted_iota(jnp.int32, (tok_count, tok_count), 1)
    after = (rows < cols).astype(jnp.bfloat16)
    earlier = jnp.dot((hot_first + hot_second).astype(jnp.bfloat16), after, preferred_element_type=jnp.float32)
    rank_first = jnp.sum(earlier * hot_first, axis=0, keepdims=True).astype(jnp.int32)
    rank_second = jnp.sum(earlier * hot_second, axis=0, keepdims=True).astype(jnp.int32)
    slot_ids = lax.broadcasted_iota(jnp.int32, (slots, tok_count), 0)
    hit_first = slot_ids == first * capacity + rank_first
    hit_second = slot_ids == second * capacity + rank_second
    gate_first = share_ref[...].astype(jnp.float32) / 16.0
    pick = (hit_first | hit_second).astype(jnp.bfloat16)
    weigh = jnp.where(hit_first, gate_first, jnp.where(hit_second, 1.0 - gate_first, 0.0)).astype(jnp.bfloat16)
    token_rows = jnp.dot(pick, normed, preferred_element_type=jnp.float32).astype(jnp.bfloat16)
    grad_rows = jnp.dot(weigh, cot_ref[...], preferred_element_type=jnp.float32).astype(jnp.bfloat16)
    send_ref[:, :capacity, :] = token_rows.reshape(experts, capacity, width)
    send_ref[:, capacity:, :] = grad_rows.reshape(experts, capacity, width)
    blank = jnp.zeros_like(pick)
    back_side_ref[:, :capacity, :] = jnp.concatenate([weigh, blank], axis=1).reshape(experts, capacity, 2 * tok_count)
    back_side_ref[:, capacity:, :] = jnp.concatenate([blank, pick], axis=1).reshape(experts, capacity, 2 * tok_count)


def prologue(tokens, cotangent, modality, modal_gains, routes, gate_share, experts, capacity):
    tok_count, width = tokens.shape
    whole = lambda shape: pl.BlockSpec(shape, lambda: (0,) * len(shape))
    return pl.pallas_call(
        lambda *refs: prologue_body(*refs, experts=experts, capacity=capacity),
        in_specs=[whole((tok_count, width)), whole((tok_count, width)), whole((1, tok_count)), whole((2, width)),
                  whole((2, tok_count)), whole((1, tok_count))],
        out_specs=[whole((experts, 2 * capacity, width)), whole((experts, 2 * capacity, 2 * tok_count))],
        out_shape=[
            jax.ShapeDtypeStruct((experts, 2 * capacity, width), jnp.bfloat16),
            jax.ShapeDtypeStruct((experts, 2 * capacity, 2 * tok_count), jnp.bfloat16),
        ],
    )(tokens, cotangent, modality.reshape(1, tok_count), modal_gains, routes.T, gate_share.reshape(1, tok_count))


def on_device(tokens, modality, modal_gains, routes, gate_share, up_weight, down_weight, cotangent):
    tok_count = tokens.shape[0]
    model_width = tokens.shape[1]
    expert_count = lax.axis_size("expert")
    replica_count = lax.axis_size("dp")
    capacity = 4 * tok_count // expert_count
    slot_count = expert_count * capacity
    route_count = 2 * tok_count
    grad_scale = 1.0 / math.sqrt(2 * tok_count * replica_count)
    whole = lax.all_gather(jnp.concatenate([up_weight, down_weight], axis=0), "dp", axis=1, tiled=True)
    sending, return_side = prologue(tokens, cotangent, modality, modal_gains, routes, gate_share, expert_count, capacity)
    arrived = lax.all_to_all(sending, "expert", split_axis=0, concat_axis=0, tiled=True)
    leaving, parts = expert_block(arrived, whole, grad_scale)
    back = lax.all_to_all(leaving, "expert", split_axis=0, concat_axis=0, tiled=True)
    parts = parts.transpose(1, 0, 2)
    grad_pair = lax.psum_scatter(parts, "dp", scatter_dimension=0, tiled=True)
    up_grad = grad_pair[:, 0][None]
    down_grad = grad_pair[:, 1][None]
    side = return_side.reshape(2 * slot_count, 2 * tok_count)
    returned = back.reshape(2 * slot_count, model_width)
    x_float = tokens.astype(jnp.float32)
    inv_rms = lax.rsqrt(jnp.mean(x_float * x_float, axis=-1, keepdims=True) + 1e-06)
    gain_rows = jnp.where(modality[:, None] == 1, modal_gains[1][None, :], modal_gains[0][None, :])
    moe_output = row_contract(side[:, :tok_count], returned).astype(jnp.bfloat16)
    normed_grad = row_contract(side[:, tok_count:], returned)
    scaled = gain_rows * normed_grad
    token_grad = (
        inv_rms * scaled - x_float * inv_rms**3 * jnp.mean(x_float * scaled, axis=-1, keepdims=True)
    ).astype(jnp.bfloat16)
    return (moe_output, token_grad, up_grad, down_grad)


def solution(mesh):
    placed = (
        P(("dp", "expert"), None),
        P(("dp", "expert")),
        P(),
        P(("dp", "expert"), None),
        P(("dp", "expert")),
        P("expert", "dp", None),
        P("expert", "dp", None),
        P(("dp", "expert"), None),
    )
    return jax.shard_map(
        on_device,
        mesh=mesh,
        in_specs=placed,
        out_specs=(
            P(("dp", "expert"), None),
            P(("dp", "expert"), None),
            P("expert", "dp", None),
            P("expert", "dp", None),
        ),
        check_vma=False,
    )
```
